768 devices in a mesh: dp: 24 (over z, y_lo), tm: 16 (over x, y_hi), rows: 2 (over core).
Axes of the slice: x: 4, y: 8 (y_hi: 4, y_lo: 2; y = y_hi * 2 + y_lo), z: 12, core: 2. Of those that a mesh axis runs over, the one named last changes fastest.
Arguments:
- queries: bfloat16 [24, 16, 1, 1, 384, 1536], P('dp', 'tm', None, None, None, 'rows'), may hold values from -44 to 44
- keys_values: bfloat16 [24, 16, 1, 1, 384, 2, 1536], P('dp', 'tm', None, None, None, None, 'rows'), may hold values from -5 to 5
- window_offsets: int32 [24, 16, 1, 1, 3], P('dp', 'tm'), may hold values from 0 to 26, as said below
- out_weight: bfloat16 [1536, 1536], P(('rows', 'dp')), may hold values from -0.15625 to 0.15625
- gate: float32 [24, 1536], P('dp'), may hold values from 3 to 30
Outputs:
- mixed: bfloat16 [24, 16, 1, 1, 384, 1536], P('dp', 'tm', None, None, 'rows')
The draws below stay inside these ranges and needn't reach their ends.
Inputs may be any that keep to these rules, and one draw needn't show every extreme that they name: `window_offsets`: entry 0 of every row is 13; the other 2 entries are distinct offsets other than 13, which may point outside the grid.
All inputs are finite; a program needn't handle non-finite values.
Results may differ from the reference program's by a relative error of at most 0.015.
Values may be sent and summed in bfloat16 or wider, within the bound.
No kernel may reach another device: no remote copies, remote signals or barrier semaphores. Data moves between devices by JAX's collectives and lax.ppermute only.
A program may use at most 64 MiB of HBM per device.

```python
import math
import jax
import jax.numpy as jnp
from jax import lax

HEADS = 12
HD = 128
C = 1536
DOUT = 1536
TL = 384
KEEP = 3
NHT = 1
WT = 1
NTT = 16
VIDEOS = 24


def draw_both(key):
    width = HEADS * HD
    shape_q = (VIDEOS, NTT, NHT, WT, TL, width)
    shape_kv = (VIDEOS, NTT, NHT, WT, TL, 2, width)
    key_q = jax.random.fold_in(key, 11)
    key_kv = jax.random.fold_in(key, 12)
    query = jnp.clip(jax.random.normal(key_q, shape_q, jnp.float32), -5.0, 5.0)
    pairs = jnp.clip(jax.random.normal(key_kv, shape_kv, jnp.float32), -5.0, 5.0)
    return (query.astype(jnp.bfloat16), pairs.astype(jnp.bfloat16))


def draw_queries(key, part):
    return draw_both(key)[0]


def draw_keys_values(key, part):
    return draw_both(key)[1]


def draw_window_offsets(key, part):
    rows_shape = (VIDEOS, NTT, NHT, WT, 26)
    scores = jax.random.randint(jax.random.fold_in(key, 21), rows_shape, 0, 1 << 20)
    scores = scores * 32 + jnp.arange(26, dtype=jnp.int32)
    order = jnp.argsort(scores, axis=-1, stable=True).astype(jnp.int32)
    others = order[..., :KEEP - 1]
    others = others + (others >= 13).astype(jnp.int32)
    centre = jnp.full((VIDEOS, NTT, NHT, WT, 1), 13, jnp.int32)
    return jnp.concatenate([centre, others], axis=-1)


def shard_levels(key, extent, cuts, least, top_value):
    factor_of = 1.0
    for position, blocks in cuts:
        heights = jax.random.uniform(jax.random.fold_in(jax.random.fold_in(key, 6), position), (blocks,), jnp.float32, least / len(cuts), top_value / len(cuts))
        factor_of = factor_of * jnp.repeat(jnp.exp(heights), extent[position] // blocks).reshape((-1,) + (1,) * (len(extent) - 1 - position))
    return factor_of


def centred(rng, dims, scale, most, cuts=(), held_as=jnp.bfloat16):
    drawn = jax.random.normal(rng, dims, jnp.float32) * scale
    if len(cuts) > 0:
        drawn = shard_levels(rng, dims, cuts, -0.22, 0.18) * drawn
    return jnp.clip(drawn, min=-most, max=most).astype(held_as)


def setup_inputs(seed: int = 0) -> dict:
    key_list = jax.random.split(jax.random.key(seed), 6)
    return {
        "queries": draw_queries(jax.random.fold_in(key_list[5], 71), 0),
        "keys_values": draw_keys_values(jax.random.fold_in(key_list[5], 71), 0),
        "window_offsets": draw_window_offsets(jax.random.fold_in(key_list[5], 71), 0),
        "out_weight": centred(key_list[3], (C, DOUT), C ** -0.5, 0.15625, ((0, 48),)),
        "gate": jnp.clip(jnp.exp(math.log(30.0) - 2.3025851 * jax.random.uniform(key_list[4], (VIDEOS, DOUT), jnp.float32) ** shard_levels(key_list[4], (VIDEOS, DOUT), ((0, 24),), -0.2, 0.2)), 3.0, 30.0),
    }


def tile_attend(query_tile, key_tiles, live_row):
    scale = float(HD) ** -0.5
    query = query_tile.astype(jnp.float32).reshape(TL, HEADS, HD)
    keys = key_tiles[:, :, 0, :].astype(jnp.float32).reshape(KEEP * TL, HEADS, HD)
    values = key_tiles[:, :, 1, :].astype(jnp.float32).reshape(KEEP * TL, HEADS, HD)
    scores = jnp.einsum("qnd,knd->nqk", query, keys) * scale
    mask = jnp.repeat(live_row, TL)[None, None, :]
    top = jnp.max(jnp.where(mask, scores, -jnp.inf), axis=2, keepdims=True)
    prob = jnp.where(mask, jnp.exp(scores - top), 0.0)
    total = jnp.sum(prob, axis=2, keepdims=True)
    weights = (prob / total).astype(jnp.bfloat16).astype(jnp.float32)
    acc = jnp.einsum("nqk,knd->qnd", weights, values)
    return acc.astype(jnp.bfloat16).reshape(TL, HEADS * HD)


def one_video(args):
    query_in, kv_in, offsets, gate_row, out_weight = args
    width = HEADS * HD
    tiles = NTT * NHT * WT
    kv_flat = kv_in.reshape(tiles, TL, 2, width)
    q_flat = query_in.reshape(tiles, TL, width)
    time_pos = jnp.arange(NTT, dtype=jnp.int32)[:, None, None, None]
    row_pos = jnp.arange(NHT, dtype=jnp.int32)[None, :, None, None]
    col_pos = jnp.arange(WT, dtype=jnp.int32)[None, None, :, None]
    first = offsets // 9 - 1
    second = (offsets // 3) % 3 - 1
    third = offsets % 3 - 1
    near_t = time_pos + first
    near_h = row_pos + second
    near_w = col_pos + third
    inside = (near_t >= 0) & (near_t < NTT) & (near_h >= 0) & (near_h < NHT) & (near_w >= 0) & (near_w < WT)
    index = (jnp.clip(near_t, 0, NTT - 1) * (NHT * WT) + jnp.clip(near_h, 0, NHT - 1) * WT + jnp.clip(near_w, 0, WT - 1)).astype(jnp.int32)
    index = index.reshape(tiles, KEEP)
    inside = inside.reshape(tiles, KEEP)

    def per_tile(items):
        query_tile, index_row, live_row = items
        key_tiles = jnp.take(kv_flat, index_row, axis=0)
        return tile_attend(query_tile, key_tiles, live_row)

    attended = lax.map(per_tile, (q_flat, index, inside)).reshape(tiles * TL, width)
    projection = jnp.dot(attended, out_weight, preferred_element_type=jnp.float32)
    mixed = (gate_row[None, :] * projection).astype(jnp.bfloat16)
    return mixed.reshape(NTT, NHT, WT, TL, DOUT)


def reference(queries, keys_values, window_offsets, out_weight, gate):
    def per_video(args):
        query_in, kv_in, offsets, gate_row = args
        return one_video((query_in, kv_in, offsets, gate_row, out_weight))
    return lax.map(per_video, (queries, keys_values, window_offsets, gate))
```

```python
import functools

import jax
import jax.numpy as jnp
from jax import lax
from jax.experimental import pallas as pl
from jax.experimental.pallas import tpu as pltpu
from jax.sharding import Mesh
from jax.sharding import PartitionSpec as P

HD = 128
DOUT = 1536

DP = ("z", "ylo")
TM = ("x", "yhi")
ROWS = "core"


def attend_kernel(flags_ref, q_ref, kvp_ref, kvc_ref, kvn_ref, o_ref):
    scale = float(HD) ** (-0.5)
    q = q_ref[...]
    tiles = (kvp_ref, kvc_ref, kvn_ref)
    scores = []
    for j, kv_ref in enumerate(tiles):
        k = kv_ref[:, 0, :]
        s = lax.dot_general(
            q, k, (((1,), (1,)), ((), ())), preferred_element_type=jnp.float32
        ) * scale
        scores.append(jnp.where(flags_ref[j] > 0, s, -jnp.inf))
    top = jnp.max(scores[0], axis=1, keepdims=True)
    for s in scores[1:]:
        top = jnp.maximum(top, jnp.max(s, axis=1, keepdims=True))
    probs = [jnp.exp(s - top) for s in scores]
    total = probs[0].sum(axis=1, keepdims=True)
    for p in probs[1:]:
        total = total + p.sum(axis=1, keepdims=True)
    inv = 1.0 / total
    acc = None
    for p, kv_ref in zip(probs, tiles):
        w = (p * inv).astype(jnp.bfloat16)
        part = jnp.dot(w, kv_ref[:, 1, :], preferred_element_type=jnp.float32)
        acc = part if acc is None else acc + part
    o_ref[...] = acc.astype(o_ref.dtype)


def attend(flags, q, kv_prev, kv_own, kv_next):
    tl, width = q.shape
    heads = width // HD
    kv_spec = pl.BlockSpec((tl, 2, HD), lambda h, f: (0, 0, h))
    grid_spec = pltpu.PrefetchScalarGridSpec(
        num_scalar_prefetch=1,
        grid=(heads,),
        in_specs=[pl.BlockSpec((tl, HD), lambda h, f: (0, h)), kv_spec, kv_spec, kv_spec],
        out_specs=pl.BlockSpec((tl, HD), lambda h, f: (0, h)),
    )
    flops = heads * 2 * 2 * tl * 3 * tl * HD
    return pl.pallas_call(
        attend_kernel,
        grid_spec=grid_spec,
        out_shape=jax.ShapeDtypeStruct((tl, width), jnp.bfloat16),
        cost_estimate=pl.CostEstimate(
            flops=flops,
            transcendentals=heads * tl * 3 * tl,
            bytes_accessed=2 * (tl * width * 2 + 3 * tl * 2 * width),
        ),
    )(flags, q, kv_prev, kv_own, kv_next)


def local(queries, keys_values, window_offsets, out_weight, gate):
    tl = queries.shape[4]
    all_time = lax.axis_size(TM)
    time_now = lax.axis_index(TM)

    forward = [(i, i + 1) for i in range(all_time - 1)]
    backward = [(i + 1, i) for i in range(all_time - 1)]
    kv = keys_values[0, 0, 0, 0]
    kv_prev = lax.ppermute(kv, TM, forward)
    kv_next = lax.ppermute(kv, TM, backward)

    head_rows = lax.all_gather(out_weight, "ylo", axis=0, tiled=True)
    head_rows = lax.all_gather(head_rows, "z", axis=0, tiled=True)

    offsets = window_offsets[0, 0, 0, 0]
    near_t = time_now + offsets // 9 - 1
    same_hw = (offsets // 3 % 3 == 1) & (offsets % 3 == 1)
    inside = same_hw & (near_t >= 0) & (near_t < all_time)
    deltas = jnp.array([-1, 0, 1], jnp.int32)
    hit = inside[None, :] & (near_t[None, :] == time_now + deltas[:, None])
    flags = jnp.any(hit, axis=1).astype(jnp.int32)

    attended = attend(flags, queries[0, 0, 0, 0], kv_prev, kv, kv_next)

    bands = lax.axis_size(ROWS)
    band = tl // bands
    me = lax.axis_index(ROWS)
    other = 1 - me
    mine_rows = lax.dynamic_slice_in_dim(attended, me * band, band, axis=0)
    other_rows = lax.dynamic_slice_in_dim(attended, other * band, band, axis=0)
    sent = jnp.dot(other_rows, head_rows, preferred_element_type=jnp.float32)
    got = lax.ppermute(sent, ROWS, [(0, 1), (1, 0)])
    kept = jnp.dot(mine_rows, head_rows, preferred_element_type=jnp.float32)
    projection = kept + got
    mixed = (gate[0][None, :] * projection).astype(jnp.bfloat16)
    return mixed.reshape(1, 1, 1, 1, band, DOUT)


def solution(mesh):
    devices = mesh.devices.reshape(12, 2, 4, 4, 2)
    fine = Mesh(devices, ("z", "ylo", "x", "yhi", "core"))
    placed = (
        P(DP, TM, None, None, None, ROWS),
        P(DP, TM, None, None, None, None, ROWS),
        P(DP, TM, None, None, None),
        P((ROWS,) + DP, None),
        P(DP, None),
    )
    return jax.shard_map(
        local,
        mesh=fine,
        in_specs=placed,
        out_specs=P(DP, TM, None, None, ROWS, None),
        check_vma=False,
    )
```

```python
import functools

import jax
import jax.numpy as jnp
from jax import lax
from jax.experimental import pallas as pl
from jax.experimental.pallas import tpu as pltpu
from jax.sharding import Mesh
from jax.sharding import PartitionSpec as P

HD = 128
DOUT = 1536

DP = ("z", "ylo")
TM = ("x", "yhi")
ROWS = "core"


def attend_kernel(flags_ref, q_ref, kvp_ref, kvc_ref, kvn_ref, o_ref):
    scale = float(HD) ** (-0.5)
    q = q_ref[...]
    tiles = (kvp_ref, kvc_ref, kvn_ref)
    scores = []
    for j, kv_ref in enumerate(tiles):
        k = kv_ref[:, 0, :]
        s = lax.dot_general(
            q, k, (((1,), (1,)), ((), ())), preferred_element_type=jnp.float32
        ) * scale
        scores.append(jnp.where(flags_ref[j] > 0, s, -jnp.inf))
    top = jnp.max(scores[0], axis=1, keepdims=True)
    for s in scores[1:]:
        top = jnp.maximum(top, jnp.max(s, axis=1, keepdims=True))
    probs = [jnp.exp(s - top) for s in scores]
    total = probs[0].sum(axis=1, keepdims=True)
    for p in probs[1:]:
        total = total + p.sum(axis=1, keepdims=True)
    inv = 1.0 / total
    acc = None
    for p, kv_ref in zip(probs, tiles):
        w = (p * inv).astype(jnp.bfloat16)
        part = jnp.dot(w, kv_ref[:, 1, :], preferred_element_type=jnp.float32)
        acc = part if acc is None else acc + part
    o_ref[...] = acc.astype(o_ref.dtype)


def attend(flags, q, kv_prev, kv_own, kv_next):
    tl, width = q.shape
    heads = width // HD
    kv_spec = pl.BlockSpec((tl, 2, HD), lambda h, f: (0, 0, h))
    grid_spec = pltpu.PrefetchScalarGridSpec(
        num_scalar_prefetch=1,
        grid=(heads,),
        in_specs=[pl.BlockSpec((tl, HD), lambda h, f: (0, h)), kv_spec, kv_spec, kv_spec],
        out_specs=pl.BlockSpec((tl, HD), lambda h, f: (0, h)),
    )
    flops = heads * 2 * 2 * tl * 3 * tl * HD
    return pl.pallas_call(
        attend_kernel,
        grid_spec=grid_spec,
        out_shape=jax.ShapeDtypeStruct((tl, width), jnp.bfloat16),
        cost_estimate=pl.CostEstimate(
            flops=flops,
            transcendentals=heads * tl * 3 * tl,
            bytes_accessed=2 * (tl * width * 2 + 3 * tl * 2 * width),
        ),
    )(flags, q, kv_prev, kv_own, kv_next)


def gather_ring(piece, axis):
    count = lax.axis_size(axis)
    here = lax.axis_index(axis)
    rows = piece.shape[0]
    whole = jnp.zeros((count * rows,) + piece.shape[1:], piece.dtype)
    whole = lax.dynamic_update_slice_in_dim(whole, piece, here * rows, axis=0)
    right = [(i, (i + 1) % count) for i in range(count)]
    left = [(i, (i - 1) % count) for i in range(count)]
    fwd = piece
    bwd = piece
    for step in range(1, count // 2 + 1):
        fwd = lax.ppermute(fwd, axis, right)
        at = (here - step + count) % count
        whole = lax.dynamic_update_slice_in_dim(whole, fwd, at * rows, axis=0)
        if step < count - step:
            bwd = lax.ppermute(bwd, axis, left)
            at = (here + step) % count
            whole = lax.dynamic_update_slice_in_dim(whole, bwd, at * rows, axis=0)
    return whole


def local(queries, keys_values, window_offsets, out_weight, gate):
    tl = queries.shape[4]
    all_time = lax.axis_size(TM)
    time_now = lax.axis_index(TM)

    forward = [(i, i + 1) for i in range(all_time - 1)]
    backward = [(i + 1, i) for i in range(all_time - 1)]
    kv = keys_values[0, 0, 0, 0]
    kv_prev = lax.ppermute(kv, TM, forward)
    kv_next = lax.ppermute(kv, TM, backward)

    pair = lax.ppermute(out_weight, "ylo", [(0, 1), (1, 0)])
    low = lax.axis_index("ylo") == 0
    head_rows = jnp.concatenate(
        [jnp.where(low, out_weight, pair), jnp.where(low, pair, out_weight)], axis=0
    )
    head_rows = gather_ring(head_rows, "z")

    offsets = window_offsets[0, 0, 0, 0]
    near_t = time_now + offsets // 9 - 1
    same_hw = (offsets // 3 % 3 == 1) & (offsets % 3 == 1)
    inside = same_hw & (near_t >= 0) & (near_t < all_time)
    deltas = jnp.array([-1, 0, 1], jnp.int32)
    hit = inside[None, :] & (near_t[None, :] == time_now + deltas[:, None])
    flags = jnp.any(hit, axis=1).astype(jnp.int32)

    attended = attend(flags, queries[0, 0, 0, 0], kv_prev, kv, kv_next)

    bands = lax.axis_size(ROWS)
    band = tl // bands
    me = lax.axis_index(ROWS)
    other = 1 - me
    mine_rows = lax.dynamic_slice_in_dim(attended, me * band, band, axis=0)
    other_rows = lax.dynamic_slice_in_dim(attended, other * band, band, axis=0)
    sent = jnp.dot(other_rows, head_rows, preferred_element_type=jnp.float32)
    got = lax.ppermute(sent, ROWS, [(0, 1), (1, 0)])
    kept = jnp.dot(mine_rows, head_rows, preferred_element_type=jnp.float32)
    kept = lax.optimization_barrier(kept)
    projection = kept + got
    mixed = (gate[0][None, :] * projection).astype(jnp.bfloat16)
    return mixed.reshape(1, 1, 1, 1, band, DOUT)


def solution(mesh):
    devices = mesh.devices.reshape(12, 2, 4, 4, 2)
    fine = Mesh(devices, ("z", "ylo", "x", "yhi", "core"))
    placed = (
        P(DP, TM, None, None, None, ROWS),
        P(DP, TM, None, None, None, None, ROWS),
        P(DP, TM, None, None, None),
        P((ROWS,) + DP, None),
        P(DP, None),
    )
    return jax.shard_map(
        local,
        mesh=fine,
        in_specs=placed,
        out_specs=P(DP, TM, None, None, ROWS, None),
        check_vma=False,
    )
```

```python
import functools

import jax
import jax.numpy as jnp
from jax import lax
from jax.experimental import pallas as pl
from jax.experimental.pallas import tpu as pltpu
from jax.sharding import Mesh
from jax.sharding import PartitionSpec as P

HD = 128
DOUT = 1536

DP = ("z", "ylo")
TM = ("x", "yhi")
ROWS = "core"
Y = ("ylo", "yhi")


def attend_kernel(flags_ref, q_ref, kvp_ref, kvc_ref, kvn_ref, o_ref):
    scale = float(HD) ** (-0.5)
    q = q_ref[...]
    tiles = (kvp_ref, kvc_ref, kvn_ref)
    scores = []
    for j, kv_ref in enumerate(tiles):
        k = kv_ref[:, 0, :]
        s = lax.dot_general(
            q, k, (((1,), (1,)), ((), ())), preferred_element_type=jnp.float32
        ) * scale
        scores.append(jnp.where(flags_ref[j] > 0, s, -jnp.inf))
    top = jnp.max(scores[0], axis=1, keepdims=True)
    for s in scores[1:]:
        top = jnp.maximum(top, jnp.max(s, axis=1, keepdims=True))
    probs = [jnp.exp(s - top) for s in scores]
    total = probs[0].sum(axis=1, keepdims=True)
    for p in probs[1:]:
        total = total + p.sum(axis=1, keepdims=True)
    inv = 1.0 / total
    acc = None
    for p, kv_ref in zip(probs, tiles):
        w = (p * inv).astype(jnp.bfloat16)
        part = jnp.dot(w, kv_ref[:, 1, :], preferred_element_type=jnp.float32)
        acc = part if acc is None else acc + part
    o_ref[...] = acc.astype(o_ref.dtype)


def attend(flags, q, kv_prev, kv_own, kv_next):
    tl, width = q.shape
    heads = width // HD
    kv_spec = pl.BlockSpec((tl, 2, HD), lambda h, f: (0, 0, h))
    grid_spec = pltpu.PrefetchScalarGridSpec(
        num_scalar_prefetch=1,
        grid=(heads,),
        in_specs=[pl.BlockSpec((tl, HD), lambda h, f: (0, h)), kv_spec, kv_spec, kv_spec],
        out_specs=pl.BlockSpec((tl, HD), lambda h, f: (0, h)),
    )
    flops = heads * 2 * 2 * tl * 3 * tl * HD
    return pl.pallas_call(
        attend_kernel,
        grid_spec=grid_spec,
        out_shape=jax.ShapeDtypeStruct((tl, width), jnp.bfloat16),
        cost_estimate=pl.CostEstimate(
            flops=flops,
            transcendentals=heads * tl * 3 * tl,
            bytes_accessed=2 * (tl * width * 2 + 3 * tl * 2 * width),
        ),
    )(flags, q, kv_prev, kv_own, kv_next)


def local(queries, keys_values, window_offsets, out_weight, gate):
    tl = queries.shape[4]
    all_time = lax.axis_size(TM)
    time_now = lax.axis_index(TM)

    forward = [(i, i + 1) for i in range(all_time - 1)]
    backward = [(i + 1, i) for i in range(all_time - 1)]
    kv = keys_values[0, 0, 0, 0]
    kv_prev = lax.ppermute(kv, TM, forward)
    kv_next = lax.ppermute(kv, TM, backward)

    own_rows = lax.all_gather(out_weight, "z", axis=0, tiled=True)

    offsets = window_offsets[0, 0, 0, 0]
    near_t = time_now + offsets // 9 - 1
    same_hw = (offsets // 3 % 3 == 1) & (offsets % 3 == 1)
    inside = same_hw & (near_t >= 0) & (near_t < all_time)
    deltas = jnp.array([-1, 0, 1], jnp.int32)
    hit = inside[None, :] & (near_t[None, :] == time_now + deltas[:, None])
    flags = jnp.any(hit, axis=1).astype(jnp.int32)

    ys = lax.axis_size(Y)
    his = lax.axis_size("yhi")
    slot = [(y % 2) * his + y // 2 for y in range(ys)]
    up = [(slot[y], slot[(y + 1) % ys]) for y in range(ys)]
    down = [(slot[y], slot[(y - 1) % ys]) for y in range(ys)]
    half = own_rows.shape[0] // 2
    own_rows, kv_prev, kv_next = lax.optimization_barrier((own_rows, kv_prev, kv_next))
    from_below = lax.ppermute(own_rows[:half], Y, up)
    from_above = lax.ppermute(own_rows[half:], Y, down)
    other_rows = jnp.concatenate([from_below, from_above], axis=0)

    attended = attend(flags, queries[0, 0, 0, 0], kv_prev, kv, kv_next)

    parity = lax.axis_index("ylo")
    zs = lax.axis_size("z")
    split = attended.reshape(tl, zs, 2, -1)
    a_own = lax.dynamic_index_in_dim(split, parity, axis=2, keepdims=False).reshape(tl, -1)
    a_other = lax.dynamic_index_in_dim(split, 1 - parity, axis=2, keepdims=False).reshape(tl, -1)

    bands = lax.axis_size(ROWS)
    band = tl // bands
    me = lax.axis_index(ROWS)

    def project(start):
        own = lax.dynamic_slice_in_dim(a_own, start, band, axis=0)
        far = lax.dynamic_slice_in_dim(a_other, start, band, axis=0)
        return jnp.dot(own, own_rows, preferred_element_type=jnp.float32) + jnp.dot(
            far, other_rows, preferred_element_type=jnp.float32
        )

    sent = project((1 - me) * band)
    got = lax.ppermute(sent, ROWS, [(0, 1), (1, 0)])
    kept = lax.optimization_barrier(project(me * band))
    projection = kept + got
    mixed = (gate[0][None, :] * projection).astype(jnp.bfloat16)
    return mixed.reshape(1, 1, 1, 1, band, DOUT)


def solution(mesh):
    devices = mesh.devices.reshape(12, 2, 4, 4, 2)
    fine = Mesh(devices, ("z", "ylo", "x", "yhi", "core"))
    placed = (
        P(DP, TM, None, None, None, ROWS),
        P(DP, TM, None, None, None, None, ROWS),
        P(DP, TM, None, None, None),
        P((ROWS,) + DP, None),
        P(DP, None),
    )
    return jax.shard_map(
        local,
        mesh=fine,
        in_specs=placed,
        out_specs=P(DP, TM, None, None, ROWS, None),
        check_vma=False,
    )
```

```python
import functools

import jax
import jax.numpy as jnp
from jax import lax
from jax.experimental import pallas as pl
from jax.experimental.pallas import tpu as pltpu
from jax.sharding import Mesh
from jax.sharding import PartitionSpec as P

HD = 128
DOUT = 1536

DP = ("z", "ylo")
TM = ("x", "yhi")
ROWS = "core"
Y = ("ylo", "yhi")


def attend_kernel(flags_ref, q_ref, kvp_ref, kvc_ref, kvn_ref, o_ref):
    scale = float(HD) ** (-0.5)
    q = q_ref[...]
    tiles = (kvp_ref, kvc_ref, kvn_ref)
    scores = []
    for j, kv_ref in enumerate(tiles):
        k = kv_ref[:, 0, :]
        s = lax.dot_general(
            q, k, (((1,), (1,)), ((), ())), preferred_element_type=jnp.float32
        ) * scale
        scores.append(jnp.where(flags_ref[j] > 0, s, -jnp.inf))
    top = jnp.max(scores[0], axis=1, keepdims=True)
    for s in scores[1:]:
        top = jnp.maximum(top, jnp.max(s, axis=1, keepdims=True))
    probs = [jnp.exp(s - top) for s in scores]
    total = probs[0].sum(axis=1, keepdims=True)
    for p in probs[1:]:
        total = total + p.sum(axis=1, keepdims=True)
    inv = 1.0 / total
    acc = None
    for p, kv_ref in zip(probs, tiles):
        w = (p * inv).astype(jnp.bfloat16)
        part = jnp.dot(w, kv_ref[:, 1, :], preferred_element_type=jnp.float32)
        acc = part if acc is None else acc + part
    o_ref[...] = acc.astype(o_ref.dtype)


def attend(flags, q, kv_prev, kv_own, kv_next):
    tl, width = q.shape
    heads = width // HD
    kv_spec = pl.BlockSpec((tl, 2, HD), lambda h, f: (0, 0, h))
    grid_spec = pltpu.PrefetchScalarGridSpec(
        num_scalar_prefetch=1,
        grid=(heads,),
        in_specs=[pl.BlockSpec((tl, HD), lambda h, f: (0, h)), kv_spec, kv_spec, kv_spec],
        out_specs=pl.BlockSpec((tl, HD), lambda h, f: (0, h)),
    )
    flops = heads * 2 * 2 * tl * 3 * tl * HD
    return pl.pallas_call(
        attend_kernel,
        grid_spec=grid_spec,
        out_shape=jax.ShapeDtypeStruct((tl, width), jnp.bfloat16),
        cost_estimate=pl.CostEstimate(
            flops=flops,
            transcendentals=heads * tl * 3 * tl,
            bytes_accessed=2 * (tl * width * 2 + 3 * tl * 2 * width),
        ),
    )(flags, q, kv_prev, kv_own, kv_next)


def gather_direct(piece, axis):
    count = lax.axis_size(axis)
    here = lax.axis_index(axis)
    rows = piece.shape[0]
    whole = jnp.zeros((count * rows,) + piece.shape[1:], piece.dtype)
    whole = lax.dynamic_update_slice_in_dim(whole, piece, here * rows, axis=0)
    for shift in range(1, count):
        moved = lax.ppermute(piece, axis, [(i, (i + shift) % count) for i in range(count)])
        at = (here - shift + count) % count
        whole = lax.dynamic_update_slice_in_dim(whole, moved, at * rows, axis=0)
    return whole


def local(queries, keys_values, window_offsets, out_weight, gate):
    tl = queries.shape[4]
    all_time = lax.axis_size(TM)
    time_now = lax.axis_index(TM)

    forward = [(i, i + 1) for i in range(all_time - 1)]
    backward = [(i + 1, i) for i in range(all_time - 1)]
    kv = keys_values[0, 0, 0, 0]
    kv_prev = lax.ppermute(kv, TM, forward)
    kv_next = lax.ppermute(kv, TM, backward)

    zs = lax.axis_size("z")
    spread = jnp.broadcast_to(out_weight[None], (zs,) + out_weight.shape)
    own_rows = lax.all_to_all(spread, "z", 0, 0, tiled=True).reshape(-1, out_weight.shape[1])

    offsets = window_offsets[0, 0, 0, 0]
    near_t = time_now + offsets // 9 - 1
    same_hw = (offsets // 3 % 3 == 1) & (offsets % 3 == 1)
    inside = same_hw & (near_t >= 0) & (near_t < all_time)
    deltas = jnp.array([-1, 0, 1], jnp.int32)
    hit = inside[None, :] & (near_t[None, :] == time_now + deltas[:, None])
    flags = jnp.any(hit, axis=1).astype(jnp.int32)

    ys = lax.axis_size(Y)
    his = lax.axis_size("yhi")
    slot = [(y % 2) * his + y // 2 for y in range(ys)]
    up = [(slot[y], slot[(y + 1) % ys]) for y in range(ys)]
    down = [(slot[y], slot[(y - 1) % ys]) for y in range(ys)]
    half = own_rows.shape[0] // 2
    own_rows, kv_prev, kv_next = lax.optimization_barrier((own_rows, kv_prev, kv_next))
    from_below = lax.ppermute(own_rows[:half], Y, up)
    from_above = lax.ppermute(own_rows[half:], Y, down)
    other_rows = jnp.concatenate([from_below, from_above], axis=0)

    attended = attend(flags, queries[0, 0, 0, 0], kv_prev, kv, kv_next)

    parity = lax.axis_index("ylo")
    split = attended.reshape(tl, zs, 2, -1)
    a_own = lax.dynamic_index_in_dim(split, parity, axis=2, keepdims=False).reshape(tl, -1)
    a_other = lax.dynamic_index_in_dim(split, 1 - parity, axis=2, keepdims=False).reshape(tl, -1)

    bands = lax.axis_size(ROWS)
    band = tl // bands
    me = lax.axis_index(ROWS)

    def project(start):
        own = lax.dynamic_slice_in_dim(a_own, start, band, axis=0)
        far = lax.dynamic_slice_in_dim(a_other, start, band, axis=0)
        return jnp.dot(own, own_rows, preferred_element_type=jnp.float32) + jnp.dot(
            far, other_rows, preferred_element_type=jnp.float32
        )

    sent = project((1 - me) * band)
    got = lax.ppermute(sent, ROWS, [(0, 1), (1, 0)])
    kept = lax.optimization_barrier(project(me * band))
    projection = kept + got
    mixed = (gate[0][None, :] * projection).astype(jnp.bfloat16)
    return mixed.reshape(1, 1, 1, 1, band, DOUT)


def solution(mesh):
    devices = mesh.devices.reshape(12, 2, 4, 4, 2)
    fine = Mesh(devices, ("z", "ylo", "x", "yhi", "core"))
    placed = (
        P(DP, TM, None, None, None, ROWS),
        P(DP, TM, None, None, None, None, ROWS),
        P(DP, TM, None, None, None),
        P((ROWS,) + DP, None),
        P(DP, None),
    )
    return jax.shard_map(
        local,
        mesh=fine,
        in_specs=placed,
        out_specs=P(DP, TM, None, None, ROWS, None),
        check_vma=False,
    )
```

```python
import functools

import jax
import jax.numpy as jnp
from jax import lax
from jax.experimental import pallas as pl
from jax.experimental.pallas import tpu as pltpu
from jax.sharding import Mesh
from jax.sharding import PartitionSpec as P

HD = 128
DOUT = 1536

DP = ("z", "ylo")
TM = ("x", "yhi")
ROWS = "core"
Y = ("ylo", "yhi")


def scores_of(q, kv_ref, live):
    scale = float(HD) ** (-0.5)
    s = lax.dot_general(
        q, kv_ref[:, 0, :], (((1,), (1,)), ((), ())), preferred_element_type=jnp.float32
    ) * scale
    return jnp.where(live, s, -jnp.inf)


def centre_kernel(flags_ref, q_ref, kv_ref, m_ref, l_ref, acc_ref):
    live = flags_ref[1] > 0
    s = scores_of(q_ref[...], kv_ref, live)
    top = jnp.max(s, axis=1, keepdims=True)
    p = jnp.where(live, jnp.exp(s - top), 0.0)
    m_ref[0] = jnp.where(live, top, -jnp.inf)
    l_ref[0] = p.sum(axis=1, keepdims=True)
    acc_ref[...] = jnp.dot(
        p.astype(jnp.bfloat16), kv_ref[:, 1, :], preferred_element_type=jnp.float32
    )


def side_kernel(flags_ref, q_ref, kvp_ref, kvn_ref, m_ref, l_ref, acc_ref, o_ref):
    q = q_ref[...]
    s_p = scores_of(q, kvp_ref, flags_ref[0] > 0)
    s_n = scores_of(q, kvn_ref, flags_ref[2] > 0)
    m_c = m_ref[0]
    top = jnp.maximum(
        m_c, jnp.maximum(jnp.max(s_p, axis=1, keepdims=True), jnp.max(s_n, axis=1, keepdims=True))
    )
    alpha = jnp.exp(m_c - top)
    p_p = jnp.exp(s_p - top)
    p_n = jnp.exp(s_n - top)
    total = alpha * l_ref[0] + p_p.sum(axis=1, keepdims=True) + p_n.sum(axis=1, keepdims=True)
    acc = alpha * acc_ref[...]
    acc = acc + jnp.dot(p_p.astype(jnp.bfloat16), kvp_ref[:, 1, :], preferred_element_type=jnp.float32)
    acc = acc + jnp.dot(p_n.astype(jnp.bfloat16), kvn_ref[:, 1, :], preferred_element_type=jnp.float32)
    o_ref[...] = (acc / total).astype(o_ref.dtype)


def attend_centre(flags, q, kv_own):
    tl, width = q.shape
    heads = width // HD
    kv_spec = pl.BlockSpec((tl, 2, HD), lambda h, f: (0, 0, h))
    q_spec = pl.BlockSpec((tl, HD), lambda h, f: (0, h))
    stat_spec = pl.BlockSpec((1, tl, 1), lambda h, f: (h, 0, 0))
    stat_shape = jax.ShapeDtypeStruct((heads, tl, 1), jnp.float32)
    tile_flops = heads * 2 * 2 * tl * tl * HD
    m_c, l_c, acc_c = pl.pallas_call(
        centre_kernel,
        grid_spec=pltpu.PrefetchScalarGridSpec(
            num_scalar_prefetch=1,
            grid=(heads,),
            in_specs=[q_spec, kv_spec],
            out_specs=[stat_spec, stat_spec, q_spec],
        ),
        out_shape=[stat_shape, stat_shape, jax.ShapeDtypeStruct((tl, width), jnp.float32)],
        cost_estimate=pl.CostEstimate(
            flops=tile_flops,
            transcendentals=heads * tl * tl,
            bytes_accessed=tl * width * 2 * 3 + tl * width * 4,
        ),
    )(flags, q, kv_own)
    return m_c, l_c, acc_c


def attend_sides(flags, q, kv_prev, kv_next, m_c, l_c, acc_c):
    tl, width = q.shape
    heads = width // HD
    kv_spec = pl.BlockSpec((tl, 2, HD), lambda h, f: (0, 0, h))
    q_spec = pl.BlockSpec((tl, HD), lambda h, f: (0, h))
    stat_spec = pl.BlockSpec((1, tl, 1), lambda h, f: (h, 0, 0))
    tile_flops = heads * 2 * 2 * tl * tl * HD
    return pl.pallas_call(
        side_kernel,
        grid_spec=pltpu.PrefetchScalarGridSpec(
            num_scalar_prefetch=1,
            grid=(heads,),
            in_specs=[q_spec, kv_spec, kv_spec, stat_spec, stat_spec, q_spec],
            out_specs=q_spec,
        ),
        out_shape=jax.ShapeDtypeStruct((tl, width), jnp.bfloat16),
        cost_estimate=pl.CostEstimate(
            flops=2 * tile_flops,
            transcendentals=2 * heads * tl * tl,
            bytes_accessed=tl * width * 2 * 6 + tl * width * 4,
        ),
    )(flags, q, kv_prev, kv_next, m_c, l_c, acc_c)


def gather_direct(piece, axis):
    count = lax.axis_size(axis)
    here = lax.axis_index(axis)
    rows = piece.shape[0]
    whole = jnp.zeros((count * rows,) + piece.shape[1:], piece.dtype)
    whole = lax.dynamic_update_slice_in_dim(whole, piece, here * rows, axis=0)
    for shift in range(1, count):
        moved = lax.ppermute(piece, axis, [(i, (i + shift) % count) for i in range(count)])
        at = (here - shift + count) % count
        whole = lax.dynamic_update_slice_in_dim(whole, moved, at * rows, axis=0)
    return whole


def local(queries, keys_values, window_offsets, out_weight, gate):
    tl = queries.shape[4]
    all_time = lax.axis_size(TM)
    time_now = lax.axis_index(TM)

    forward = [(i, i + 1) for i in range(all_time - 1)]
    backward = [(i + 1, i) for i in range(all_time - 1)]
    kv = keys_values[0, 0, 0, 0]
    kv_prev = lax.ppermute(kv, TM, forward)
    kv_next = lax.ppermute(kv, TM, backward)

    zs = lax.axis_size("z")
    spread = jnp.broadcast_to(out_weight[None], (zs,) + out_weight.shape)
    own_rows = lax.all_to_all(spread, "z", 0, 0, tiled=True).reshape(-1, out_weight.shape[1])

    offsets = window_offsets[0, 0, 0, 0]
    near_t = time_now + offsets // 9 - 1
    same_hw = (offsets // 3 % 3 == 1) & (offsets % 3 == 1)
    inside = same_hw & (near_t >= 0) & (near_t < all_time)
    deltas = jnp.array([-1, 0, 1], jnp.int32)
    hit = inside[None, :] & (near_t[None, :] == time_now + deltas[:, None])
    flags = jnp.any(hit, axis=1).astype(jnp.int32)

    ys = lax.axis_size(Y)
    his = lax.axis_size("yhi")
    slot = [(y % 2) * his + y // 2 for y in range(ys)]
    up = [(slot[y], slot[(y + 1) % ys]) for y in range(ys)]
    down = [(slot[y], slot[(y - 1) % ys]) for y in range(ys)]
    half = own_rows.shape[0] // 2
    q = queries[0, 0, 0, 0]
    centre = attend_centre(flags, q, kv)
    own_rows, kv_prev, kv_next, centre = lax.optimization_barrier(
        (own_rows, kv_prev, kv_next, centre)
    )
    from_below = lax.ppermute(own_rows[:half], Y, up)
    from_above = lax.ppermute(own_rows[half:], Y, down)

    attended = attend_sides(flags, q, kv_prev, kv_next, *centre)

    parity = lax.axis_index("ylo")
    split = attended.reshape(tl, zs, 2, -1)
    a_own = lax.dynamic_index_in_dim(split, parity, axis=2, keepdims=False).reshape(tl, -1)
    a_other = lax.dynamic_index_in_dim(split, 1 - parity, axis=2, keepdims=False).reshape(tl, -1)

    bands = lax.axis_size(ROWS)
    band = tl // bands
    me = lax.axis_index(ROWS)

    def project(start):
        own = lax.dynamic_slice_in_dim(a_own, start, band, axis=0)
        far = lax.dynamic_slice_in_dim(a_other, start, band, axis=0)
        part = jnp.dot(own, own_rows, preferred_element_type=jnp.float32)
        part = part + jnp.dot(far[:, :half], from_below, preferred_element_type=jnp.float32)
        return part + jnp.dot(far[:, half:], from_above, preferred_element_type=jnp.float32)

    sent = project((1 - me) * band)
    got = lax.ppermute(sent, ROWS, [(0, 1), (1, 0)])
    kept = lax.optimization_barrier(project(me * band))
    projection = kept + got
    mixed = (gate[0][None, :] * projection).astype(jnp.bfloat16)
    return mixed.reshape(1, 1, 1, 1, band, DOUT)


def solution(mesh):
    devices = mesh.devices.reshape(12, 2, 4, 4, 2)
    fine = Mesh(devices, ("z", "ylo", "x", "yhi", "core"))
    placed = (
        P(DP, TM, None, None, None, ROWS),
        P(DP, TM, None, None, None, None, ROWS),
        P(DP, TM, None, None, None),
        P((ROWS,) + DP, None),
        P(DP, None),
    )
    return jax.shard_map(
        local,
        mesh=fine,
        in_specs=placed,
        out_specs=P(DP, TM, None, None, ROWS, None),
        check_vma=False,
    )
```

```python
import functools

import jax
import jax.numpy as jnp
from jax import lax
from jax.experimental import pallas as pl
from jax.experimental.pallas import tpu as pltpu
from jax.sharding import Mesh
from jax.sharding import PartitionSpec as P

HD = 128
DOUT = 1536

DP = ("z", "ylo")
TM = ("x", "yhi")
ROWS = "core"


def scores_of(q, kv_ref, live):
    scale = float(HD) ** (-0.5)
    s = lax.dot_general(
        q, kv_ref[:, 0, :], (((1,), (1,)), ((), ())), preferred_element_type=jnp.float32
    ) * scale
    return jnp.where(live, s, -jnp.inf)


def centre_kernel(flags_ref, q_ref, kv_ref, m_ref, l_ref, acc_ref):
    live = flags_ref[1] > 0
    s = scores_of(q_ref[...], kv_ref, live)
    top = jnp.max(s, axis=1, keepdims=True)
    p = jnp.where(live, jnp.exp(s - top), 0.0)
    m_ref[0] = jnp.where(live, top, -jnp.inf)
    l_ref[0] = p.sum(axis=1, keepdims=True)
    acc_ref[...] = jnp.dot(
        p.astype(jnp.bfloat16), kv_ref[:, 1, :], preferred_element_type=jnp.float32
    )


def side_kernel(flags_ref, q_ref, kvp_ref, kvn_ref, m_ref, l_ref, acc_ref, o_ref):
    q = q_ref[...]
    s_p = scores_of(q, kvp_ref, flags_ref[0] > 0)
    s_n = scores_of(q, kvn_ref, flags_ref[2] > 0)
    m_c = m_ref[0]
    top = jnp.maximum(
        m_c, jnp.maximum(jnp.max(s_p, axis=1, keepdims=True), jnp.max(s_n, axis=1, keepdims=True))
    )
    alpha = jnp.exp(m_c - top)
    p_p = jnp.exp(s_p - top)
    p_n = jnp.exp(s_n - top)
    total = alpha * l_ref[0] + p_p.sum(axis=1, keepdims=True) + p_n.sum(axis=1, keepdims=True)
    acc = alpha * acc_ref[...]
    acc = acc + jnp.dot(p_p.astype(jnp.bfloat16), kvp_ref[:, 1, :], preferred_element_type=jnp.float32)
    acc = acc + jnp.dot(p_n.astype(jnp.bfloat16), kvn_ref[:, 1, :], preferred_element_type=jnp.float32)
    o_ref[...] = (acc / total).astype(o_ref.dtype)


def attend_centre(flags, q, kv_own):
    tl, width = q.shape
    heads = width // HD
    kv_spec = pl.BlockSpec((tl, 2, HD), lambda h, f: (0, 0, h))
    q_spec = pl.BlockSpec((tl, HD), lambda h, f: (0, h))
    stat_spec = pl.BlockSpec((1, tl, 1), lambda h, f: (h, 0, 0))
    stat_shape = jax.ShapeDtypeStruct((heads, tl, 1), jnp.float32)
    tile_flops = heads * 2 * 2 * tl * tl * HD
    m_c, l_c, acc_c = pl.pallas_call(
        centre_kernel,
        grid_spec=pltpu.PrefetchScalarGridSpec(
            num_scalar_prefetch=1,
            grid=(heads,),
            in_specs=[q_spec, kv_spec],
            out_specs=[stat_spec, stat_spec, q_spec],
        ),
        out_shape=[stat_shape, stat_shape, jax.ShapeDtypeStruct((tl, width), jnp.float32)],
        cost_estimate=pl.CostEstimate(
            flops=tile_flops,
            transcendentals=heads * tl * tl,
            bytes_accessed=tl * width * 2 * 3 + tl * width * 4,
        ),
    )(flags, q, kv_own)
    return m_c, l_c, acc_c


def attend_sides(flags, q, kv_prev, kv_next, m_c, l_c, acc_c):
    tl, width = q.shape
    heads = width // HD
    kv_spec = pl.BlockSpec((tl, 2, HD), lambda h, f: (0, 0, h))
    q_spec = pl.BlockSpec((tl, HD), lambda h, f: (0, h))
    stat_spec = pl.BlockSpec((1, tl, 1), lambda h, f: (h, 0, 0))
    tile_flops = heads * 2 * 2 * tl * tl * HD
    return pl.pallas_call(
        side_kernel,
        grid_spec=pltpu.PrefetchScalarGridSpec(
            num_scalar_prefetch=1,
            grid=(heads,),
            in_specs=[q_spec, kv_spec, kv_spec, stat_spec, stat_spec, q_spec],
            out_specs=q_spec,
        ),
        out_shape=jax.ShapeDtypeStruct((tl, width), jnp.bfloat16),
        cost_estimate=pl.CostEstimate(
            flops=2 * tile_flops,
            transcendentals=2 * heads * tl * tl,
            bytes_accessed=tl * width * 2 * 6 + tl * width * 4,
        ),
    )(flags, q, kv_prev, kv_next, m_c, l_c, acc_c)


def local(queries, keys_values, window_offsets, out_weight, gate):
    tl = queries.shape[4]
    all_time = lax.axis_size(TM)
    time_now = lax.axis_index(TM)

    pair = lax.ppermute(out_weight, "ylo", [(0, 1), (1, 0)])
    low = lax.axis_index("ylo") == 0
    both = jnp.concatenate(
        [jnp.where(low, out_weight, pair), jnp.where(low, pair, out_weight)], axis=0
    )
    kv = keys_values[0, 0, 0, 0]
    kv, both = lax.optimization_barrier((kv, both))

    forward = [(i, i + 1) for i in range(all_time - 1)]
    backward = [(i + 1, i) for i in range(all_time - 1)]
    kv_prev = lax.ppermute(kv, TM, forward)
    kv_next = lax.ppermute(kv, TM, backward)

    zs = lax.axis_size("z")
    spread = jnp.broadcast_to(both[None], (zs,) + both.shape)
    head_rows = lax.all_to_all(spread, "z", 0, 0, tiled=True).reshape(-1, both.shape[1])

    offsets = window_offsets[0, 0, 0, 0]
    near_t = time_now + offsets // 9 - 1
    same_hw = (offsets // 3 % 3 == 1) & (offsets % 3 == 1)
    inside = same_hw & (near_t >= 0) & (near_t < all_time)
    deltas = jnp.array([-1, 0, 1], jnp.int32)
    hit = inside[None, :] & (near_t[None, :] == time_now + deltas[:, None])
    flags = jnp.any(hit, axis=1).astype(jnp.int32)

    q = queries[0, 0, 0, 0]
    centre = attend_centre(flags, q, kv)
    kv_prev, kv_next, centre = lax.optimization_barrier((kv_prev, kv_next, centre))
    attended = attend_sides(flags, q, kv_prev, kv_next, *centre)

    bands = lax.axis_size(ROWS)
    band = tl // bands
    me = lax.axis_index(ROWS)
    mine_rows = lax.dynamic_slice_in_dim(attended, me * band, band, axis=0)
    other_rows = lax.dynamic_slice_in_dim(attended, (1 - me) * band, band, axis=0)
    sent = jnp.dot(other_rows, head_rows, preferred_element_type=jnp.float32)
    got = lax.ppermute(sent, ROWS, [(0, 1), (1, 0)])
    kept = jnp.dot(mine_rows, head_rows, preferred_element_type=jnp.float32)
    kept = lax.optimization_barrier(kept)
    projection = kept + got
    mixed = (gate[0][None, :] * projection).astype(jnp.bfloat16)
    return mixed.reshape(1, 1, 1, 1, band, DOUT)


def solution(mesh):
    devices = mesh.devices.reshape(12, 2, 4, 4, 2)
    fine = Mesh(devices, ("z", "ylo", "x", "yhi", "core"))
    placed = (
        P(DP, TM, None, None, None, ROWS),
        P(DP, TM, None, None, None, None, ROWS),
        P(DP, TM, None, None, None),
        P((ROWS,) + DP, None),
        P(DP, None),
    )
    return jax.shard_map(
        local,
        mesh=fine,
        in_specs=placed,
        out_specs=P(DP, TM, None, None, ROWS, None),
        check_vma=False,
    )
```

```python
import functools

import jax
import jax.numpy as jnp
from jax import lax
from jax.experimental import pallas as pl
from jax.experimental.pallas import tpu as pltpu
from jax.sharding import Mesh
from jax.sharding import PartitionSpec as P

HD = 128
DOUT = 1536

DP = ("z", "ylo")
TM = ("x", "yhi")
ROWS = "core"
Y = ("ylo", "yhi")


def scores_of(q, k_ref, live):
    scale = float(HD) ** (-0.5)
    s = lax.dot_general(
        q, k_ref[...], (((1,), (1,)), ((), ())), preferred_element_type=jnp.float32
    ) * scale
    return jnp.where(live, s, -jnp.inf)


def centre_kernel(flags_ref, q_ref, k_ref, v_ref, m_ref, l_ref, acc_ref):
    live = flags_ref[1] > 0
    s = scores_of(q_ref[...], k_ref, live)
    top = jnp.max(s, axis=1, keepdims=True)
    p = jnp.where(live, jnp.exp(s - top), 0.0)
    m_ref[0] = jnp.where(live, top, -jnp.inf)
    l_ref[0] = p.sum(axis=1, keepdims=True)
    acc_ref[...] = jnp.dot(
        p.astype(jnp.bfloat16), v_ref[...], preferred_element_type=jnp.float32
    )


def side_kernel(flags_ref, q_ref, kp_ref, vp_ref, kn_ref, vn_ref, m_ref, l_ref, acc_ref, o_ref):
    q = q_ref[...]
    s_p = scores_of(q, kp_ref, flags_ref[0] > 0)
    s_n = scores_of(q, kn_ref, flags_ref[2] > 0)
    m_c = m_ref[0]
    top = jnp.maximum(
        m_c, jnp.maximum(jnp.max(s_p, axis=1, keepdims=True), jnp.max(s_n, axis=1, keepdims=True))
    )
    alpha = jnp.exp(m_c - top)
    p_p = jnp.exp(s_p - top)
    p_n = jnp.exp(s_n - top)
    total = alpha * l_ref[0] + p_p.sum(axis=1, keepdims=True) + p_n.sum(axis=1, keepdims=True)
    acc = alpha * acc_ref[...]
    acc = acc + jnp.dot(p_p.astype(jnp.bfloat16), vp_ref[...], preferred_element_type=jnp.float32)
    acc = acc + jnp.dot(p_n.astype(jnp.bfloat16), vn_ref[...], preferred_element_type=jnp.float32)
    o_ref[...] = (acc / total).astype(o_ref.dtype)


def split_kernel(kv_ref, o_ref):
    o_ref[0] = kv_ref[:, 0, :]
    o_ref[1] = kv_ref[:, 1, :]


def split_keys_values(kv):
    tl, _, width = kv.shape
    return pl.pallas_call(
        split_kernel,
        grid=(width // HD,),
        in_specs=[pl.BlockSpec((tl, 2, HD), lambda h: (0, 0, h))],
        out_specs=pl.BlockSpec((2, tl, HD), lambda h: (0, 0, h)),
        out_shape=jax.ShapeDtypeStruct((2, tl, width), kv.dtype),
        cost_estimate=pl.CostEstimate(flops=0, transcendentals=0, bytes_accessed=4 * tl * width * 2),
    )(kv)


def attend_centre(flags, q, kv_own):
    tl, width = q.shape
    heads = width // HD
    k_spec = pl.BlockSpec((None, tl, HD), lambda h, f: (0, 0, h))
    v_spec = pl.BlockSpec((None, tl, HD), lambda h, f: (1, 0, h))
    q_spec = pl.BlockSpec((tl, HD), lambda h, f: (0, h))
    stat_spec = pl.BlockSpec((1, tl, 1), lambda h, f: (h, 0, 0))
    stat_shape = jax.ShapeDtypeStruct((heads, tl, 1), jnp.float32)
    tile_flops = heads * 2 * 2 * tl * tl * HD
    m_c, l_c, acc_c = pl.pallas_call(
        centre_kernel,
        grid_spec=pltpu.PrefetchScalarGridSpec(
            num_scalar_prefetch=1,
            grid=(heads,),
            in_specs=[q_spec, k_spec, v_spec],
            out_specs=[stat_spec, stat_spec, q_spec],
        ),
        out_shape=[stat_shape, stat_shape, jax.ShapeDtypeStruct((tl, width), jnp.float32)],
        cost_estimate=pl.CostEstimate(
            flops=tile_flops,
            transcendentals=heads * tl * tl,
            bytes_accessed=tl * width * 2 * 3 + tl * width * 4,
        ),
    )(flags, q, kv_own, kv_own)
    return m_c, l_c, acc_c


def attend_sides(flags, q, kv_prev, kv_next, m_c, l_c, acc_c):
    tl, width = q.shape
    heads = width // HD
    k_spec = pl.BlockSpec((None, tl, HD), lambda h, f: (0, 0, h))
    v_spec = pl.BlockSpec((None, tl, HD), lambda h, f: (1, 0, h))
    q_spec = pl.BlockSpec((tl, HD), lambda h, f: (0, h))
    stat_spec = pl.BlockSpec((1, tl, 1), lambda h, f: (h, 0, 0))
    tile_flops = heads * 2 * 2 * tl * tl * HD
    return pl.pallas_call(
        side_kernel,
        grid_spec=pltpu.PrefetchScalarGridSpec(
            num_scalar_prefetch=1,
            grid=(heads,),
            in_specs=[q_spec, k_spec, v_spec, k_spec, v_spec, stat_spec, stat_spec, q_spec],
            out_specs=q_spec,
        ),
        out_shape=jax.ShapeDtypeStruct((tl, width), jnp.bfloat16),
        cost_estimate=pl.CostEstimate(
            flops=2 * tile_flops,
            transcendentals=2 * heads * tl * tl,
            bytes_accessed=tl * width * 2 * 6 + tl * width * 4,
        ),
    )(flags, q, kv_prev, kv_prev, kv_next, kv_next, m_c, l_c, acc_c)


def local(queries, keys_values, window_offsets, out_weight, gate):
    tl = queries.shape[4]
    all_time = lax.axis_size(TM)
    time_now = lax.axis_index(TM)

    forward = [(i, i + 1) for i in range(all_time - 1)]
    backward = [(i + 1, i) for i in range(all_time - 1)]
    kv = split_keys_values(keys_values[0, 0, 0, 0])
    kv_prev = lax.ppermute(kv, TM, forward)
    kv_next = lax.ppermute(kv, TM, backward)

    zs = lax.axis_size("z")
    spread = jnp.broadcast_to(out_weight[None], (zs,) + out_weight.shape)
    own_rows = lax.all_to_all(spread, "z", 0, 0, tiled=True).reshape(-1, out_weight.shape[1])

    offsets = window_offsets[0, 0, 0, 0]
    near_t = time_now + offsets // 9 - 1
    same_hw = (offsets // 3 % 3 == 1) & (offsets % 3 == 1)
    inside = same_hw & (near_t >= 0) & (near_t < all_time)
    deltas = jnp.array([-1, 0, 1], jnp.int32)
    hit = inside[None, :] & (near_t[None, :] == time_now + deltas[:, None])
    flags = jnp.any(hit, axis=1).astype(jnp.int32)

    ys = lax.axis_size(Y)
    his = lax.axis_size("yhi")
    slot = [(y % 2) * his + y // 2 for y in range(ys)]
    up = [(slot[y], slot[(y + 1) % ys]) for y in range(ys)]
    down = [(slot[y], slot[(y - 1) % ys]) for y in range(ys)]
    half = own_rows.shape[0] // 2
    q = queries[0, 0, 0, 0]
    centre = attend_centre(flags, q, kv)
    own_rows, kv_prev, kv_next, centre = lax.optimization_barrier(
        (own_rows, kv_prev, kv_next, centre)
    )
    from_below = lax.ppermute(own_rows[:half], Y, up)
    from_above = lax.ppermute(own_rows[half:], Y, down)

    attended = attend_sides(flags, q, kv_prev, kv_next, *centre)

    parity = lax.axis_index("ylo")
    split = attended.reshape(tl, zs, 2, -1)
    a_own = lax.dynamic_index_in_dim(split, parity, axis=2, keepdims=False).reshape(tl, -1)
    a_other = lax.dynamic_index_in_dim(split, 1 - parity, axis=2, keepdims=False).reshape(tl, -1)

    bands = lax.axis_size(ROWS)
    band = tl // bands
    me = lax.axis_index(ROWS)

    def project(start):
        own = lax.dynamic_slice_in_dim(a_own, start, band, axis=0)
        far = lax.dynamic_slice_in_dim(a_other, start, band, axis=0)
        part = jnp.dot(own, own_rows, preferred_element_type=jnp.float32)
        part = part + jnp.dot(far[:, :half], from_below, preferred_element_type=jnp.float32)
        return part + jnp.dot(far[:, half:], from_above, preferred_element_type=jnp.float32)

    sent = project((1 - me) * band)
    got = lax.ppermute(sent, ROWS, [(0, 1), (1, 0)])
    kept = lax.optimization_barrier(project(me * band))
    projection = kept + got
    mixed = (gate[0][None, :] * projection).astype(jnp.bfloat16)
    return mixed.reshape(1, 1, 1, 1, band, DOUT)


def solution(mesh):
    devices = mesh.devices.reshape(12, 2, 4, 4, 2)
    fine = Mesh(devices, ("z", "ylo", "x", "yhi", "core"))
    placed = (
        P(DP, TM, None, None, None, ROWS),
        P(DP, TM, None, None, None, None, ROWS),
        P(DP, TM, None, None, None),
        P((ROWS,) + DP, None),
        P(DP, None),
    )
    return jax.shard_map(
        local,
        mesh=fine,
        in_specs=placed,
        out_specs=P(DP, TM, None, None, ROWS, None),
        check_vma=False,
    )
```

```python
import functools

import jax
import jax.numpy as jnp
from jax import lax
from jax.experimental import pallas as pl
from jax.experimental.pallas import tpu as pltpu
from jax.sharding import Mesh
from jax.sharding import PartitionSpec as P

HD = 128
DOUT = 1536

DP = ("z", "ylo")
TM = ("x", "yhi")
ROWS = "core"
Y = ("ylo", "yhi")


def scores_of(q, k_ref, live):
    scale = float(HD) ** (-0.5)
    s = lax.dot_general(
        q, k_ref[...], (((1,), (1,)), ((), ())), preferred_element_type=jnp.float32
    ) * scale
    return jnp.where(live, s, -jnp.inf)


def centre_kernel(flags_ref, q_ref, k_ref, v_ref, m_ref, l_ref, acc_ref):
    live = flags_ref[1] > 0
    s = scores_of(q_ref[...], k_ref, live)
    top = jnp.max(s, axis=1, keepdims=True)
    p = jnp.where(live, jnp.exp(s - top), 0.0)
    m_ref[0] = jnp.where(live, top, -jnp.inf)
    l_ref[0] = p.sum(axis=1, keepdims=True)
    acc_ref[...] = jnp.dot(
        p.astype(jnp.bfloat16), v_ref[...], preferred_element_type=jnp.float32
    )


def side_kernel(flags_ref, q_ref, kp_ref, vp_ref, kn_ref, vn_ref, m_ref, l_ref, acc_ref, o_ref):
    q = q_ref[...]
    s_p = scores_of(q, kp_ref, flags_ref[0] > 0)
    s_n = scores_of(q, kn_ref, flags_ref[2] > 0)
    m_c = m_ref[0]
    top = jnp.maximum(
        m_c, jnp.maximum(jnp.max(s_p, axis=1, keepdims=True), jnp.max(s_n, axis=1, keepdims=True))
    )
    alpha = jnp.exp(m_c - top)
    p_p = jnp.exp(s_p - top)
    p_n = jnp.exp(s_n - top)
    total = alpha * l_ref[0] + p_p.sum(axis=1, keepdims=True) + p_n.sum(axis=1, keepdims=True)
    acc = alpha * acc_ref[...]
    acc = acc + jnp.dot(p_p.astype(jnp.bfloat16), vp_ref[...], preferred_element_type=jnp.float32)
    acc = acc + jnp.dot(p_n.astype(jnp.bfloat16), vn_ref[...], preferred_element_type=jnp.float32)
    o_ref[...] = (acc / total).astype(o_ref.dtype)


def split_kernel(kv_ref, o_ref):
    o_ref[...] = jnp.swapaxes(kv_ref[...], 0, 1)


def split_keys_values(kv):
    tl, _, width = kv.shape
    return pl.pallas_call(
        split_kernel,
        grid=(width // HD,),
        in_specs=[pl.BlockSpec((tl, 2, HD), lambda h: (0, 0, h))],
        out_specs=pl.BlockSpec((2, tl, HD), lambda h: (0, 0, h)),
        out_shape=jax.ShapeDtypeStruct((2, tl, width), kv.dtype),
        cost_estimate=pl.CostEstimate(flops=0, transcendentals=0, bytes_accessed=4 * tl * width * 2),
    )(kv)


def attend_centre(flags, q, kv_own):
    tl, width = q.shape
    heads = width // HD
    k_spec = pl.BlockSpec((None, tl, HD), lambda h, f: (0, 0, h))
    v_spec = pl.BlockSpec((None, tl, HD), lambda h, f: (1, 0, h))
    q_spec = pl.BlockSpec((tl, HD), lambda h, f: (0, h))
    stat_spec = pl.BlockSpec((1, tl, 1), lambda h, f: (h, 0, 0))
    stat_shape = jax.ShapeDtypeStruct((heads, tl, 1), jnp.float32)
    tile_flops = heads * 2 * 2 * tl * tl * HD
    m_c, l_c, acc_c = pl.pallas_call(
        centre_kernel,
        grid_spec=pltpu.PrefetchScalarGridSpec(
            num_scalar_prefetch=1,
            grid=(heads,),
            in_specs=[q_spec, k_spec, v_spec],
            out_specs=[stat_spec, stat_spec, q_spec],
        ),
        out_shape=[stat_shape, stat_shape, jax.ShapeDtypeStruct((tl, width), jnp.float32)],
        cost_estimate=pl.CostEstimate(
            flops=tile_flops,
            transcendentals=heads * tl * tl,
            bytes_accessed=tl * width * 2 * 3 + tl * width * 4,
        ),
    )(flags, q, kv_own, kv_own)
    return m_c, l_c, acc_c


def attend_sides(flags, q, kv_prev, kv_next, m_c, l_c, acc_c):
    tl, width = q.shape
    heads = width // HD
    k_spec = pl.BlockSpec((None, tl, HD), lambda h, f: (0, 0, h))
    v_spec = pl.BlockSpec((None, tl, HD), lambda h, f: (1, 0, h))
    q_spec = pl.BlockSpec((tl, HD), lambda h, f: (0, h))
    stat_spec = pl.BlockSpec((1, tl, 1), lambda h, f: (h, 0, 0))
    tile_flops = heads * 2 * 2 * tl * tl * HD
    return pl.pallas_call(
        side_kernel,
        grid_spec=pltpu.PrefetchScalarGridSpec(
            num_scalar_prefetch=1,
            grid=(heads,),
            in_specs=[q_spec, k_spec, v_spec, k_spec, v_spec, stat_spec, stat_spec, q_spec],
            out_specs=q_spec,
        ),
        out_shape=jax.ShapeDtypeStruct((tl, width), jnp.bfloat16),
        cost_estimate=pl.CostEstimate(
            flops=2 * tile_flops,
            transcendentals=2 * heads * tl * tl,
            bytes_accessed=tl * width * 2 * 6 + tl * width * 4,
        ),
    )(flags, q, kv_prev, kv_prev, kv_next, kv_next, m_c, l_c, acc_c)


def local(queries, keys_values, window_offsets, out_weight, gate):
    tl = queries.shape[4]
    all_time = lax.axis_size(TM)
    time_now = lax.axis_index(TM)

    forward = [(i, i + 1) for i in range(all_time - 1)]
    backward = [(i + 1, i) for i in range(all_time - 1)]
    kv = split_keys_values(keys_values[0, 0, 0, 0])
    kv_prev = lax.ppermute(kv, TM, forward)
    kv_next = lax.ppermute(kv, TM, backward)

    zs = lax.axis_size("z")
    spread = jnp.broadcast_to(out_weight[None], (zs,) + out_weight.shape)
    own_rows = lax.all_to_all(spread, "z", 0, 0, tiled=True).reshape(-1, out_weight.shape[1])

    offsets = window_offsets[0, 0, 0, 0]
    near_t = time_now + offsets // 9 - 1
    same_hw = (offsets // 3 % 3 == 1) & (offsets % 3 == 1)
    inside = same_hw & (near_t >= 0) & (near_t < all_time)
    deltas = jnp.array([-1, 0, 1], jnp.int32)
    hit = inside[None, :] & (near_t[None, :] == time_now + deltas[:, None])
    flags = jnp.any(hit, axis=1).astype(jnp.int32)

    ys = lax.axis_size(Y)
    his = lax.axis_size("yhi")
    slot = [(y % 2) * his + y // 2 for y in range(ys)]
    up = [(slot[y], slot[(y + 1) % ys]) for y in range(ys)]
    down = [(slot[y], slot[(y - 1) % ys]) for y in range(ys)]
    half = own_rows.shape[0] // 2
    q = queries[0, 0, 0, 0]
    centre = attend_centre(flags, q, kv)
    own_rows, kv_prev, kv_next, centre = lax.optimization_barrier(
        (own_rows, kv_prev, kv_next, centre)
    )
    from_below = lax.ppermute(own_rows[:half], Y, up)
    from_above = lax.ppermute(own_rows[half:], Y, down)

    attended = attend_sides(flags, q, kv_prev, kv_next, *centre)

    parity = lax.axis_index("ylo")
    split = attended.reshape(tl, zs, 2, -1)
    a_own = lax.dynamic_index_in_dim(split, parity, axis=2, keepdims=False).reshape(tl, -1)
    a_other = lax.dynamic_index_in_dim(split, 1 - parity, axis=2, keepdims=False).reshape(tl, -1)

    bands = lax.axis_size(ROWS)
    band = tl // bands
    me = lax.axis_index(ROWS)

    def project(start):
        own = lax.dynamic_slice_in_dim(a_own, start, band, axis=0)
        far = lax.dynamic_slice_in_dim(a_other, start, band, axis=0)
        part = jnp.dot(own, own_rows, preferred_element_type=jnp.float32)
        part = part + jnp.dot(far[:, :half], from_below, preferred_element_type=jnp.float32)
        return part + jnp.dot(far[:, half:], from_above, preferred_element_type=jnp.float32)

    sent = project((1 - me) * band)
    got = lax.ppermute(sent, ROWS, [(0, 1), (1, 0)])
    kept = lax.optimization_barrier(project(me * band))
    projection = kept + got
    mixed = (gate[0][None, :] * projection).astype(jnp.bfloat16)
    return mixed.reshape(1, 1, 1, 1, band, DOUT)


def solution(mesh):
    devices = mesh.devices.reshape(12, 2, 4, 4, 2)
    fine = Mesh(devices, ("z", "ylo", "x", "yhi", "core"))
    placed = (
        P(DP, TM, None, None, None, ROWS),
        P(DP, TM, None, None, None, None, ROWS),
        P(DP, TM, None, None, None),
        P((ROWS,) + DP, None),
        P(DP, None),
    )
    return jax.shard_map(
        local,
        mesh=fine,
        in_specs=placed,
        out_specs=P(DP, TM, None, None, ROWS, None),
        check_vma=False,
    )
```

```python
import functools

import jax
import jax.numpy as jnp
from jax import lax
from jax.experimental import pallas as pl
from jax.experimental.pallas import tpu as pltpu
from jax.sharding import Mesh
from jax.sharding import PartitionSpec as P

HD = 128
DOUT = 1536

DP = ("z", "ylo")
TM = ("x", "yhi")
ROWS = "core"
Y = ("ylo", "yhi")


def scores_of(q, k_ref, live):
    scale = float(HD) ** (-0.5)
    s = lax.dot_general(
        q, k_ref[...], (((1,), (1,)), ((), ())), preferred_element_type=jnp.float32
    ) * scale
    return jnp.where(live, s, -jnp.inf)


def centre_kernel(flags_ref, q_ref, k_ref, v_ref, m_ref, l_ref, acc_ref):
    live = flags_ref[1] > 0
    s = scores_of(q_ref[...], k_ref, live)
    top = jnp.max(s, axis=1, keepdims=True)
    p = jnp.where(live, jnp.exp(s - top), 0.0)
    m_ref[0] = jnp.where(live, top, -jnp.inf)
    l_ref[0] = p.sum(axis=1, keepdims=True)
    acc_ref[...] = jnp.dot(
        p.astype(jnp.bfloat16), v_ref[...], preferred_element_type=jnp.float32
    )


def side_kernel(flags_ref, q_ref, kp_ref, vp_ref, kn_ref, vn_ref, m_ref, l_ref, acc_ref, o_ref):
    q = q_ref[...]
    s_p = scores_of(q, kp_ref, flags_ref[0] > 0)
    s_n = scores_of(q, kn_ref, flags_ref[2] > 0)
    m_c = m_ref[0]
    top = jnp.maximum(
        m_c, jnp.maximum(jnp.max(s_p, axis=1, keepdims=True), jnp.max(s_n, axis=1, keepdims=True))
    )
    alpha = jnp.exp(m_c - top)
    p_p = jnp.exp(s_p - top)
    p_n = jnp.exp(s_n - top)
    total = alpha * l_ref[0] + p_p.sum(axis=1, keepdims=True) + p_n.sum(axis=1, keepdims=True)
    acc = alpha * acc_ref[...]
    acc = acc + jnp.dot(p_p.astype(jnp.bfloat16), vp_ref[...], preferred_element_type=jnp.float32)
    acc = acc + jnp.dot(p_n.astype(jnp.bfloat16), vn_ref[...], preferred_element_type=jnp.float32)
    o_ref[...] = (acc / total).astype(o_ref.dtype)


def split_kernel(kv_ref, o_ref):
    o_ref[...] = jnp.swapaxes(kv_ref[...], 0, 1)


def split_keys_values(kv):
    tl, _, width = kv.shape
    return pl.pallas_call(
        split_kernel,
        in_specs=[pl.BlockSpec(memory_space=pltpu.VMEM)],
        out_specs=pl.BlockSpec(memory_space=pltpu.VMEM),
        out_shape=jax.ShapeDtypeStruct((2, tl, width), kv.dtype),
        cost_estimate=pl.CostEstimate(flops=0, transcendentals=0, bytes_accessed=4 * tl * width * 2),
    )(kv)


def attend_centre(flags, q, kv_own):
    tl, width = q.shape
    heads = width // HD
    k_spec = pl.BlockSpec((None, tl, HD), lambda h, f: (0, 0, h))
    v_spec = pl.BlockSpec((None, tl, HD), lambda h, f: (1, 0, h))
    q_spec = pl.BlockSpec((tl, HD), lambda h, f: (0, h))
    stat_spec = pl.BlockSpec((1, tl, 1), lambda h, f: (h, 0, 0))
    stat_shape = jax.ShapeDtypeStruct((heads, tl, 1), jnp.float32)
    tile_flops = heads * 2 * 2 * tl * tl * HD
    m_c, l_c, acc_c = pl.pallas_call(
        centre_kernel,
        grid_spec=pltpu.PrefetchScalarGridSpec(
            num_scalar_prefetch=1,
            grid=(heads,),
            in_specs=[q_spec, k_spec, v_spec],
            out_specs=[stat_spec, stat_spec, q_spec],
        ),
        out_shape=[stat_shape, stat_shape, jax.ShapeDtypeStruct((tl, width), jnp.float32)],
        cost_estimate=pl.CostEstimate(
            flops=tile_flops,
            transcendentals=heads * tl * tl,
            bytes_accessed=tl * width * 2 * 3 + tl * width * 4,
        ),
    )(flags, q, kv_own, kv_own)
    return m_c, l_c, acc_c


def attend_sides(flags, q, kv_prev, kv_next, m_c, l_c, acc_c):
    tl, width = q.shape
    heads = width // HD
    k_spec = pl.BlockSpec((None, tl, HD), lambda h, f: (0, 0, h))
    v_spec = pl.BlockSpec((None, tl, HD), lambda h, f: (1, 0, h))
    q_spec = pl.BlockSpec((tl, HD), lambda h, f: (0, h))
    stat_spec = pl.BlockSpec((1, tl, 1), lambda h, f: (h, 0, 0))
    tile_flops = heads * 2 * 2 * tl * tl * HD
    return pl.pallas_call(
        side_kernel,
        grid_spec=pltpu.PrefetchScalarGridSpec(
            num_scalar_prefetch=1,
            grid=(heads,),
            in_specs=[q_spec, k_spec, v_spec, k_spec, v_spec, stat_spec, stat_spec, q_spec],
            out_specs=q_spec,
        ),
        out_shape=jax.ShapeDtypeStruct((tl, width), jnp.bfloat16),
        cost_estimate=pl.CostEstimate(
            flops=2 * tile_flops,
            transcendentals=2 * heads * tl * tl,
            bytes_accessed=tl * width * 2 * 6 + tl * width * 4,
        ),
    )(flags, q, kv_prev, kv_prev, kv_next, kv_next, m_c, l_c, acc_c)


def local(queries, keys_values, window_offsets, out_weight, gate):
    tl = queries.shape[4]
    all_time = lax.axis_size(TM)
    time_now = lax.axis_index(TM)

    forward = [(i, i + 1) for i in range(all_time - 1)]
    backward = [(i + 1, i) for i in range(all_time - 1)]
    kv = split_keys_values(keys_values[0, 0, 0, 0])
    kv_prev = lax.ppermute(kv, TM, forward)
    kv_next = lax.ppermute(kv, TM, backward)

    zs = lax.axis_size("z")
    spread = jnp.broadcast_to(out_weight[None], (zs,) + out_weight.shape)
    spread, kv = lax.optimization_barrier((spread, kv))
    own_rows = lax.all_to_all(spread, "z", 0, 0, tiled=True).reshape(-1, out_weight.shape[1])

    offsets = window_offsets[0, 0, 0, 0]
    near_t = time_now + offsets // 9 - 1
    same_hw = (offsets // 3 % 3 == 1) & (offsets % 3 == 1)
    inside = same_hw & (near_t >= 0) & (near_t < all_time)
    deltas = jnp.array([-1, 0, 1], jnp.int32)
    hit = inside[None, :] & (near_t[None, :] == time_now + deltas[:, None])
    flags = jnp.any(hit, axis=1).astype(jnp.int32)

    ys = lax.axis_size(Y)
    his = lax.axis_size("yhi")
    slot = [(y % 2) * his + y // 2 for y in range(ys)]
    up = [(slot[y], slot[(y + 1) % ys]) for y in range(ys)]
    down = [(slot[y], slot[(y - 1) % ys]) for y in range(ys)]
    half = own_rows.shape[0] // 2
    q = queries[0, 0, 0, 0]
    centre = attend_centre(flags, q, kv)
    own_rows, kv_prev, kv_next, centre = lax.optimization_barrier(
        (own_rows, kv_prev, kv_next, centre)
    )
    from_below = lax.ppermute(own_rows[:half], Y, up)
    from_above = lax.ppermute(own_rows[half:], Y, down)

    attended = attend_sides(flags, q, kv_prev, kv_next, *centre)

    parity = lax.axis_index("ylo")
    split = attended.reshape(tl, zs, 2, -1)
    a_own = lax.dynamic_index_in_dim(split, parity, axis=2, keepdims=False).reshape(tl, -1)
    a_other = lax.dynamic_index_in_dim(split, 1 - parity, axis=2, keepdims=False).reshape(tl, -1)

    bands = lax.axis_size(ROWS)
    band = tl // bands
    me = lax.axis_index(ROWS)

    def project(start):
        own = lax.dynamic_slice_in_dim(a_own, start, band, axis=0)
        far = lax.dynamic_slice_in_dim(a_other, start, band, axis=0)
        part = jnp.dot(own, own_rows, preferred_element_type=jnp.float32)
        part = part + jnp.dot(far[:, :half], from_below, preferred_element_type=jnp.float32)
        return part + jnp.dot(far[:, half:], from_above, preferred_element_type=jnp.float32)

    sent = project((1 - me) * band)
    got = lax.ppermute(sent, ROWS, [(0, 1), (1, 0)])
    kept = lax.optimization_barrier(project(me * band))
    projection = kept + got
    mixed = (gate[0][None, :] * projection).astype(jnp.bfloat16)
    return mixed.reshape(1, 1, 1, 1, band, DOUT)


def solution(mesh):
    devices = mesh.devices.reshape(12, 2, 4, 4, 2)
    fine = Mesh(devices, ("z", "ylo", "x", "yhi", "core"))
    placed = (
        P(DP, TM, None, None, None, ROWS),
        P(DP, TM, None, None, None, None, ROWS),
        P(DP, TM, None, None, None),
        P((ROWS,) + DP, None),
        P(DP, None),
    )
    return jax.shard_map(
        local,
        mesh=fine,
        in_specs=placed,
        out_specs=P(DP, TM, None, None, ROWS, None),
        check_vma=False,
    )
```

```python
import functools

import jax
import jax.numpy as jnp
from jax import lax
from jax.experimental import pallas as pl
from jax.experimental.pallas import tpu as pltpu
from jax.sharding import Mesh
from jax.sharding import PartitionSpec as P

HD = 128
DOUT = 1536

DP = ("z", "ylo")
TM = ("x", "yhi")
ROWS = "core"
Y = ("ylo", "yhi")


def scores_of(q, k_ref, live):
    scale = float(HD) ** (-0.5)
    s = lax.dot_general(
        q, k_ref[...], (((1,), (1,)), ((), ())), preferred_element_type=jnp.float32
    ) * scale
    return jnp.where(live, s, -jnp.inf)


def centre_kernel(flags_ref, q_ref, k_ref, v_ref, m_ref, l_ref, acc_ref):
    live = flags_ref[1] > 0
    s = scores_of(q_ref[...], k_ref, live)
    top = jnp.max(s, axis=1, keepdims=True)
    p = jnp.where(live, jnp.exp(s - top), 0.0)
    m_ref[0] = jnp.where(live, top, -jnp.inf)
    l_ref[0] = p.sum(axis=1, keepdims=True)
    acc_ref[...] = jnp.dot(
        p.astype(jnp.bfloat16), v_ref[...], preferred_element_type=jnp.float32
    )


def side_kernel(flags_ref, q_ref, kp_ref, vp_ref, kn_ref, vn_ref, m_ref, l_ref, acc_ref, o_ref):
    q = q_ref[...]
    s_p = scores_of(q, kp_ref, flags_ref[0] > 0)
    s_n = scores_of(q, kn_ref, flags_ref[2] > 0)
    m_c = m_ref[0]
    top = jnp.maximum(
        m_c, jnp.maximum(jnp.max(s_p, axis=1, keepdims=True), jnp.max(s_n, axis=1, keepdims=True))
    )
    alpha = jnp.exp(m_c - top)
    p_p = jnp.exp(s_p - top)
    p_n = jnp.exp(s_n - top)
    total = alpha * l_ref[0] + p_p.sum(axis=1, keepdims=True) + p_n.sum(axis=1, keepdims=True)
    acc = alpha * acc_ref[...]
    acc = acc + jnp.dot(p_p.astype(jnp.bfloat16), vp_ref[...], preferred_element_type=jnp.float32)
    acc = acc + jnp.dot(p_n.astype(jnp.bfloat16), vn_ref[...], preferred_element_type=jnp.float32)
    o_ref[...] = (acc / total).astype(o_ref.dtype)


def split_kernel(kv_ref, o_ref):
    o_ref[...] = jnp.swapaxes(kv_ref[...], 0, 1)


def split_keys_values(kv):
    tl, _, width = kv.shape
    return pl.pallas_call(
        split_kernel,
        in_specs=[pl.BlockSpec(memory_space=pltpu.VMEM)],
        out_specs=pl.BlockSpec(memory_space=pltpu.VMEM),
        out_shape=jax.ShapeDtypeStruct((2, tl, width), kv.dtype),
        cost_estimate=pl.CostEstimate(flops=0, transcendentals=0, bytes_accessed=4 * tl * width * 2),
    )(kv)


def attend_centre(flags, q, kv_own):
    tl, width = q.shape
    heads = width // HD
    k_spec = pl.BlockSpec((None, tl, HD), lambda h, f: (0, 0, h))
    v_spec = pl.BlockSpec((None, tl, HD), lambda h, f: (1, 0, h))
    q_spec = pl.BlockSpec((tl, HD), lambda h, f: (0, h))
    stat_spec = pl.BlockSpec((1, tl, 1), lambda h, f: (h, 0, 0))
    stat_shape = jax.ShapeDtypeStruct((heads, tl, 1), jnp.float32)
    tile_flops = heads * 2 * 2 * tl * tl * HD
    m_c, l_c, acc_c = pl.pallas_call(
        centre_kernel,
        grid_spec=pltpu.PrefetchScalarGridSpec(
            num_scalar_prefetch=1,
            grid=(heads,),
            in_specs=[q_spec, k_spec, v_spec],
            out_specs=[stat_spec, stat_spec, q_spec],
        ),
        out_shape=[stat_shape, stat_shape, jax.ShapeDtypeStruct((tl, width), jnp.float32)],
        cost_estimate=pl.CostEstimate(
            flops=tile_flops,
            transcendentals=heads * tl * tl,
            bytes_accessed=tl * width * 2 * 3 + tl * width * 4,
        ),
    )(flags, q, kv_own, kv_own)
    return m_c, l_c, acc_c


def attend_sides(flags, q, kv_prev, kv_next, m_c, l_c, acc_c):
    tl, width = q.shape
    heads = width // HD
    k_spec = pl.BlockSpec((None, tl, HD), lambda h, f: (0, 0, h))
    v_spec = pl.BlockSpec((None, tl, HD), lambda h, f: (1, 0, h))
    q_spec = pl.BlockSpec((tl, HD), lambda h, f: (0, h))
    stat_spec = pl.BlockSpec((1, tl, 1), lambda h, f: (h, 0, 0))
    tile_flops = heads * 2 * 2 * tl * tl * HD
    return pl.pallas_call(
        side_kernel,
        grid_spec=pltpu.PrefetchScalarGridSpec(
            num_scalar_prefetch=1,
            grid=(heads,),
            in_specs=[q_spec, k_spec, v_spec, k_spec, v_spec, stat_spec, stat_spec, q_spec],
            out_specs=q_spec,
        ),
        out_shape=jax.ShapeDtypeStruct((tl, width), jnp.bfloat16),
        cost_estimate=pl.CostEstimate(
            flops=2 * tile_flops,
            transcendentals=2 * heads * tl * tl,
            bytes_accessed=tl * width * 2 * 6 + tl * width * 4,
        ),
    )(flags, q, kv_prev, kv_prev, kv_next, kv_next, m_c, l_c, acc_c)


def local(queries, keys_values, window_offsets, out_weight, gate):
    tl = queries.shape[4]
    all_time = lax.axis_size(TM)
    time_now = lax.axis_index(TM)

    forward = [(i, i + 1) for i in range(all_time - 1)]
    backward = [(i + 1, i) for i in range(all_time - 1)]
    kv = split_keys_values(keys_values[0, 0, 0, 0])
    kv_prev = lax.ppermute(kv, TM, forward)
    kv_next = lax.ppermute(kv, TM, backward)

    zs = lax.axis_size("z")
    own_rows = lax.all_gather(out_weight, "z", axis=0, tiled=True)

    offsets = window_offsets[0, 0, 0, 0]
    near_t = time_now + offsets // 9 - 1
    same_hw = (offsets // 3 % 3 == 1) & (offsets % 3 == 1)
    inside = same_hw & (near_t >= 0) & (near_t < all_time)
    deltas = jnp.array([-1, 0, 1], jnp.int32)
    hit = inside[None, :] & (near_t[None, :] == time_now + deltas[:, None])
    flags = jnp.any(hit, axis=1).astype(jnp.int32)

    ys = lax.axis_size(Y)
    his = lax.axis_size("yhi")
    slot = [(y % 2) * his + y // 2 for y in range(ys)]
    up = [(slot[y], slot[(y + 1) % ys]) for y in range(ys)]
    down = [(slot[y], slot[(y - 1) % ys]) for y in range(ys)]
    half = own_rows.shape[0] // 2
    q = queries[0, 0, 0, 0]
    centre = attend_centre(flags, q, kv)
    own_rows, kv_prev, kv_next, centre = lax.optimization_barrier(
        (own_rows, kv_prev, kv_next, centre)
    )
    from_below = lax.ppermute(own_rows[:half], Y, up)
    from_above = lax.ppermute(own_rows[half:], Y, down)

    attended = attend_sides(flags, q, kv_prev, kv_next, *centre)

    parity = lax.axis_index("ylo")
    split = attended.reshape(tl, zs, 2, -1)
    a_own = lax.dynamic_index_in_dim(split, parity, axis=2, keepdims=False).reshape(tl, -1)
    a_other = lax.dynamic_index_in_dim(split, 1 - parity, axis=2, keepdims=False).reshape(tl, -1)

    bands = lax.axis_size(ROWS)
    band = tl // bands
    me = lax.axis_index(ROWS)

    def project(start):
        own = lax.dynamic_slice_in_dim(a_own, start, band, axis=0)
        far = lax.dynamic_slice_in_dim(a_other, start, band, axis=0)
        part = jnp.dot(own, own_rows, preferred_element_type=jnp.float32)
        part = part + jnp.dot(far[:, :half], from_below, preferred_element_type=jnp.float32)
        return part + jnp.dot(far[:, half:], from_above, preferred_element_type=jnp.float32)

    sent = project((1 - me) * band)
    got = lax.ppermute(sent, ROWS, [(0, 1), (1, 0)])
    kept = lax.optimization_barrier(project(me * band))
    projection = kept + got
    mixed = (gate[0][None, :] * projection).astype(jnp.bfloat16)
    return mixed.reshape(1, 1, 1, 1, band, DOUT)


def solution(mesh):
    devices = mesh.devices.reshape(12, 2, 4, 4, 2)
    fine = Mesh(devices, ("z", "ylo", "x", "yhi", "core"))
    placed = (
        P(DP, TM, None, None, None, ROWS),
        P(DP, TM, None, None, None, None, ROWS),
        P(DP, TM, None, None, None),
        P((ROWS,) + DP, None),
        P(DP, None),
    )
    return jax.shard_map(
        local,
        mesh=fine,
        in_specs=placed,
        out_specs=P(DP, TM, None, None, ROWS, None),
        check_vma=False,
    )
```

```python
import functools

import jax
import jax.numpy as jnp
from jax import lax
from jax.experimental import pallas as pl
from jax.experimental.pallas import tpu as pltpu
from jax.sharding import Mesh
from jax.sharding import PartitionSpec as P

HD = 128
DOUT = 1536

DP = ("z", "ylo")
TM = ("x", "yhi")
ROWS = "core"
Y = ("ylo", "yhi")


def scores_of(q, k_ref, live):
    scale = float(HD) ** (-0.5)
    s = lax.dot_general(
        q, k_ref[...], (((1,), (1,)), ((), ())), preferred_element_type=jnp.float32
    ) * scale
    return jnp.where(live, s, -jnp.inf)


def centre_kernel(flags_ref, q_ref, k_ref, v_ref, m_ref, l_ref, acc_ref):
    live = flags_ref[1] > 0
    s = scores_of(q_ref[...], k_ref, live)
    top = jnp.max(s, axis=1, keepdims=True)
    p = jnp.where(live, jnp.exp(s - top), 0.0)
    m_ref[0] = jnp.where(live, top, -jnp.inf)
    l_ref[0] = p.sum(axis=1, keepdims=True)
    acc_ref[...] = jnp.dot(
        p.astype(jnp.bfloat16), v_ref[...], preferred_element_type=jnp.float32
    )


def side_kernel(flags_ref, q_ref, kp_ref, vp_ref, kn_ref, vn_ref, m_ref, l_ref, acc_ref, o_ref):
    q = q_ref[...]
    s_p = scores_of(q, kp_ref, flags_ref[0] > 0)
    s_n = scores_of(q, kn_ref, flags_ref[2] > 0)
    m_c = m_ref[0]
    top = jnp.maximum(
        m_c, jnp.maximum(jnp.max(s_p, axis=1, keepdims=True), jnp.max(s_n, axis=1, keepdims=True))
    )
    alpha = jnp.exp(m_c - top)
    p_p = jnp.exp(s_p - top)
    p_n = jnp.exp(s_n - top)
    total = alpha * l_ref[0] + p_p.sum(axis=1, keepdims=True) + p_n.sum(axis=1, keepdims=True)
    acc = alpha * acc_ref[...]
    acc = acc + jnp.dot(p_p.astype(jnp.bfloat16), vp_ref[...], preferred_element_type=jnp.float32)
    acc = acc + jnp.dot(p_n.astype(jnp.bfloat16), vn_ref[...], preferred_element_type=jnp.float32)
    o_ref[...] = (acc / total).astype(o_ref.dtype)


def split_kernel(kv_ref, o_ref):
    o_ref[...] = jnp.swapaxes(kv_ref[...], 0, 1)


def split_keys_values(kv):
    tl, _, width = kv.shape
    return pl.pallas_call(
        split_kernel,
        in_specs=[pl.BlockSpec(memory_space=pltpu.VMEM)],
        out_specs=pl.BlockSpec(memory_space=pltpu.VMEM),
        out_shape=jax.ShapeDtypeStruct((2, tl, width), kv.dtype),
        cost_estimate=pl.CostEstimate(flops=0, transcendentals=0, bytes_accessed=4 * tl * width * 2),
    )(kv)


def attend_centre(flags, q, kv_own):
    tl, width = q.shape
    heads = width // HD
    k_spec = pl.BlockSpec((None, tl, HD), lambda h, f: (0, 0, h))
    v_spec = pl.BlockSpec((None, tl, HD), lambda h, f: (1, 0, h))
    q_spec = pl.BlockSpec((tl, HD), lambda h, f: (0, h))
    stat_spec = pl.BlockSpec((1, tl, 1), lambda h, f: (h, 0, 0))
    stat_shape = jax.ShapeDtypeStruct((heads, tl, 1), jnp.float32)
    tile_flops = heads * 2 * 2 * tl * tl * HD
    m_c, l_c, acc_c = pl.pallas_call(
        centre_kernel,
        grid_spec=pltpu.PrefetchScalarGridSpec(
            num_scalar_prefetch=1,
            grid=(heads,),
            in_specs=[q_spec, k_spec, v_spec],
            out_specs=[stat_spec, stat_spec, q_spec],
        ),
        out_shape=[stat_shape, stat_shape, jax.ShapeDtypeStruct((tl, width), jnp.float32)],
        cost_estimate=pl.CostEstimate(
            flops=tile_flops,
            transcendentals=heads * tl * tl,
            bytes_accessed=tl * width * 2 * 3 + tl * width * 4,
        ),
    )(flags, q, kv_own, kv_own)
    return m_c, l_c, acc_c


def attend_sides(flags, q, kv_prev, kv_next, m_c, l_c, acc_c):
    tl, width = q.shape
    heads = width // HD
    k_spec = pl.BlockSpec((None, tl, HD), lambda h, f: (0, 0, h))
    v_spec = pl.BlockSpec((None, tl, HD), lambda h, f: (1, 0, h))
    q_spec = pl.BlockSpec((tl, HD), lambda h, f: (0, h))
    stat_spec = pl.BlockSpec((1, tl, 1), lambda h, f: (h, 0, 0))
    tile_flops = heads * 2 * 2 * tl * tl * HD
    return pl.pallas_call(
        side_kernel,
        grid_spec=pltpu.PrefetchScalarGridSpec(
            num_scalar_prefetch=1,
            grid=(heads,),
            in_specs=[q_spec, k_spec, v_spec, k_spec, v_spec, stat_spec, stat_spec, q_spec],
            out_specs=q_spec,
        ),
        out_shape=jax.ShapeDtypeStruct((tl, width), jnp.bfloat16),
        cost_estimate=pl.CostEstimate(
            flops=2 * tile_flops,
            transcendentals=2 * heads * tl * tl,
            bytes_accessed=tl * width * 2 * 6 + tl * width * 4,
        ),
    )(flags, q, kv_prev, kv_prev, kv_next, kv_next, m_c, l_c, acc_c)


def shifted(x, axis, count, shift):
    return lax.ppermute(x, axis, [(i, (i + shift) % count) for i in range(count)])


def gather_two_rounds(piece, axis):
    count = lax.axis_size(axis)
    here = lax.axis_index(axis)
    rows = piece.shape[0]
    block = jnp.concatenate(
        [shifted(piece, axis, count, 1), piece, shifted(piece, axis, count, -1)], axis=0
    )
    whole = jnp.zeros((count * rows,) + piece.shape[1:], piece.dtype)
    for shift in (0, 3, -3, 6):
        moved = block if shift == 0 else shifted(block, axis, count, shift)
        for j in range(3):
            at = (here - shift + j - 1 + 2 * count) % count
            whole = lax.dynamic_update_slice_in_dim(
                whole, moved[j * rows:(j + 1) * rows], at * rows, axis=0
            )
    return whole


def local(queries, keys_values, window_offsets, out_weight, gate):
    tl = queries.shape[4]
    all_time = lax.axis_size(TM)
    time_now = lax.axis_index(TM)

    forward = [(i, i + 1) for i in range(all_time - 1)]
    backward = [(i + 1, i) for i in range(all_time - 1)]
    kv = split_keys_values(keys_values[0, 0, 0, 0])
    kv_prev = lax.ppermute(kv, TM, forward)
    kv_next = lax.ppermute(kv, TM, backward)

    zs = lax.axis_size("z")
    piece, kv = lax.optimization_barrier((out_weight, kv))
    own_rows = gather_two_rounds(piece, "z")

    offsets = window_offsets[0, 0, 0, 0]
    near_t = time_now + offsets // 9 - 1
    same_hw = (offsets // 3 % 3 == 1) & (offsets % 3 == 1)
    inside = same_hw & (near_t >= 0) & (near_t < all_time)
    deltas = jnp.array([-1, 0, 1], jnp.int32)
    hit = inside[None, :] & (near_t[None, :] == time_now + deltas[:, None])
    flags = jnp.any(hit, axis=1).astype(jnp.int32)

    ys = lax.axis_size(Y)
    his = lax.axis_size("yhi")
    slot = [(y % 2) * his + y // 2 for y in range(ys)]
    up = [(slot[y], slot[(y + 1) % ys]) for y in range(ys)]
    down = [(slot[y], slot[(y - 1) % ys]) for y in range(ys)]
    half = own_rows.shape[0] // 2
    q = queries[0, 0, 0, 0]
    centre = attend_centre(flags, q, kv)
    own_rows, kv_prev, kv_next, centre = lax.optimization_barrier(
        (own_rows, kv_prev, kv_next, centre)
    )
    from_below = lax.ppermute(own_rows[:half], Y, up)
    from_above = lax.ppermute(own_rows[half:], Y, down)

    attended = attend_sides(flags, q, kv_prev, kv_next, *centre)

    parity = lax.axis_index("ylo")
    split = attended.reshape(tl, zs, 2, -1)
    a_own = lax.dynamic_index_in_dim(split, parity, axis=2, keepdims=False).reshape(tl, -1)
    a_other = lax.dynamic_index_in_dim(split, 1 - parity, axis=2, keepdims=False).reshape(tl, -1)

    bands = lax.axis_size(ROWS)
    band = tl // bands
    me = lax.axis_index(ROWS)

    def project(start):
        own = lax.dynamic_slice_in_dim(a_own, start, band, axis=0)
        far = lax.dynamic_slice_in_dim(a_other, start, band, axis=0)
        part = jnp.dot(own, own_rows, preferred_element_type=jnp.float32)
        part = part + jnp.dot(far[:, :half], from_below, preferred_element_type=jnp.float32)
        return part + jnp.dot(far[:, half:], from_above, preferred_element_type=jnp.float32)

    sent = project((1 - me) * band)
    got = lax.ppermute(sent, ROWS, [(0, 1), (1, 0)])
    kept = lax.optimization_barrier(project(me * band))
    projection = kept + got
    mixed = (gate[0][None, :] * projection).astype(jnp.bfloat16)
    return mixed.reshape(1, 1, 1, 1, band, DOUT)


def solution(mesh):
    devices = mesh.devices.reshape(12, 2, 4, 4, 2)
    fine = Mesh(devices, ("z", "ylo", "x", "yhi", "core"))
    placed = (
        P(DP, TM, None, None, None, ROWS),
        P(DP, TM, None, None, None, None, ROWS),
        P(DP, TM, None, None, None),
        P((ROWS,) + DP, None),
        P(DP, None),
    )
    return jax.shard_map(
        local,
        mesh=fine,
        in_specs=placed,
        out_specs=P(DP, TM, None, None, ROWS, None),
        check_vma=False,
    )
```

```python
import functools

import jax
import jax.numpy as jnp
from jax import lax
from jax.experimental import pallas as pl
from jax.experimental.pallas import tpu as pltpu
from jax.sharding import Mesh
from jax.sharding import PartitionSpec as P

HD = 128
DOUT = 1536

DP = ("z", "ylo")
TM = ("x", "yhi")
ROWS = "core"
Y = ("ylo", "yhi")


def scores_of(q, k_ref, live):
    scale = float(HD) ** (-0.5)
    s = lax.dot_general(
        q, k_ref[...], (((1,), (1,)), ((), ())), preferred_element_type=jnp.float32
    ) * scale
    return jnp.where(live, s, -jnp.inf)


def centre_kernel(flags_ref, q_ref, k_ref, v_ref, m_ref, l_ref, acc_ref):
    live = flags_ref[1] > 0
    s = scores_of(q_ref[...], k_ref, live)
    top = jnp.max(s, axis=1, keepdims=True)
    p = jnp.where(live, jnp.exp(s - top), 0.0)
    m_ref[0] = jnp.where(live, top, -jnp.inf)
    l_ref[0] = p.sum(axis=1, keepdims=True)
    acc_ref[...] = jnp.dot(
        p.astype(jnp.bfloat16), v_ref[...], preferred_element_type=jnp.float32
    )


def side_kernel(flags_ref, q_ref, kp_ref, vp_ref, kn_ref, vn_ref, m_ref, l_ref, acc_ref, o_ref):
    q = q_ref[...]
    s_p = scores_of(q, kp_ref, flags_ref[0] > 0)
    s_n = scores_of(q, kn_ref, flags_ref[2] > 0)
    m_c = m_ref[0]
    top = jnp.maximum(
        m_c, jnp.maximum(jnp.max(s_p, axis=1, keepdims=True), jnp.max(s_n, axis=1, keepdims=True))
    )
    alpha = jnp.exp(m_c - top)
    p_p = jnp.exp(s_p - top)
    p_n = jnp.exp(s_n - top)
    total = alpha * l_ref[0] + p_p.sum(axis=1, keepdims=True) + p_n.sum(axis=1, keepdims=True)
    acc = alpha * acc_ref[...]
    acc = acc + jnp.dot(p_p.astype(jnp.bfloat16), vp_ref[...], preferred_element_type=jnp.float32)
    acc = acc + jnp.dot(p_n.astype(jnp.bfloat16), vn_ref[...], preferred_element_type=jnp.float32)
    o_ref[...] = (acc / total).astype(o_ref.dtype)


def split_kernel(kv_ref, o_ref):
    o_ref[...] = jnp.swapaxes(kv_ref[...], 0, 1)


def split_keys_values(kv):
    tl, _, width = kv.shape
    return pl.pallas_call(
        split_kernel,
        in_specs=[pl.BlockSpec(memory_space=pltpu.VMEM)],
        out_specs=pl.BlockSpec(memory_space=pltpu.VMEM),
        out_shape=jax.ShapeDtypeStruct((2, tl, width), kv.dtype),
        cost_estimate=pl.CostEstimate(flops=0, transcendentals=0, bytes_accessed=4 * tl * width * 2),
    )(kv)


def attend_centre(flags, q, kv_own):
    tl, width = q.shape
    heads = width // HD
    k_spec = pl.BlockSpec((None, tl, HD), lambda h, f: (0, 0, h))
    v_spec = pl.BlockSpec((None, tl, HD), lambda h, f: (1, 0, h))
    q_spec = pl.BlockSpec((tl, HD), lambda h, f: (0, h))
    stat_spec = pl.BlockSpec((1, tl, 1), lambda h, f: (h, 0, 0))
    stat_shape = jax.ShapeDtypeStruct((heads, tl, 1), jnp.float32)
    tile_flops = heads * 2 * 2 * tl * tl * HD
    m_c, l_c, acc_c = pl.pallas_call(
        centre_kernel,
        grid_spec=pltpu.PrefetchScalarGridSpec(
            num_scalar_prefetch=1,
            grid=(heads,),
            in_specs=[q_spec, k_spec, v_spec],
            out_specs=[stat_spec, stat_spec, q_spec],
        ),
        out_shape=[stat_shape, stat_shape, jax.ShapeDtypeStruct((tl, width), jnp.float32)],
        cost_estimate=pl.CostEstimate(
            flops=tile_flops,
            transcendentals=heads * tl * tl,
            bytes_accessed=tl * width * 2 * 3 + tl * width * 4,
        ),
    )(flags, q, kv_own, kv_own)
    return m_c, l_c, acc_c


def attend_sides(flags, q, kv_prev, kv_next, m_c, l_c, acc_c):
    tl, width = q.shape
    heads = width // HD
    k_spec = pl.BlockSpec((None, tl, HD), lambda h, f: (0, 0, h))
    v_spec = pl.BlockSpec((None, tl, HD), lambda h, f: (1, 0, h))
    q_spec = pl.BlockSpec((tl, HD), lambda h, f: (0, h))
    stat_spec = pl.BlockSpec((1, tl, 1), lambda h, f: (h, 0, 0))
    tile_flops = heads * 2 * 2 * tl * tl * HD
    return pl.pallas_call(
        side_kernel,
        grid_spec=pltpu.PrefetchScalarGridSpec(
            num_scalar_prefetch=1,
            grid=(heads,),
            in_specs=[q_spec, k_spec, v_spec, k_spec, v_spec, stat_spec, stat_spec, q_spec],
            out_specs=q_spec,
        ),
        out_shape=jax.ShapeDtypeStruct((tl, width), jnp.bfloat16),
        cost_estimate=pl.CostEstimate(
            flops=2 * tile_flops,
            transcendentals=2 * heads * tl * tl,
            bytes_accessed=tl * width * 2 * 6 + tl * width * 4,
        ),
    )(flags, q, kv_prev, kv_prev, kv_next, kv_next, m_c, l_c, acc_c)


def local(queries, keys_values, window_offsets, out_weight, gate):
    tl = queries.shape[4]
    all_time = lax.axis_size(TM)
    time_now = lax.axis_index(TM)

    forward = [(i, i + 1) for i in range(all_time - 1)]
    backward = [(i + 1, i) for i in range(all_time - 1)]
    kv = split_keys_values(keys_values[0, 0, 0, 0])
    kv_prev = lax.ppermute(kv, TM, forward)
    kv_next = lax.ppermute(kv, TM, backward)

    zs = lax.axis_size("z")
    spread = jnp.broadcast_to(out_weight[None], (zs,) + out_weight.shape)
    spread, kv = lax.optimization_barrier((spread, kv))
    own_rows = lax.all_to_all(spread, "z", 0, 0, tiled=True).reshape(-1, out_weight.shape[1])

    offsets = window_offsets[0, 0, 0, 0]
    near_t = time_now + offsets // 9 - 1
    same_hw = (offsets // 3 % 3 == 1) & (offsets % 3 == 1)
    inside = same_hw & (near_t >= 0) & (near_t < all_time)
    deltas = jnp.array([-1, 0, 1], jnp.int32)
    hit = inside[None, :] & (near_t[None, :] == time_now + deltas[:, None])
    flags = jnp.any(hit, axis=1).astype(jnp.int32)

    ys = lax.axis_size(Y)
    his = lax.axis_size("yhi")
    slot = [(y % 2) * his + y // 2 for y in range(ys)]
    up = [(slot[y], slot[(y + 1) % ys]) for y in range(ys)]
    down = [(slot[y], slot[(y - 1) % ys]) for y in range(ys)]
    half = own_rows.shape[0] // 2
    q = queries[0, 0, 0, 0]
    centre = attend_centre(flags, q, kv)
    own_rows, kv_prev, kv_next, centre = lax.optimization_barrier(
        (own_rows, kv_prev, kv_next, centre)
    )
    from_below = lax.ppermute(own_rows[:half], Y, up)
    from_above = lax.ppermute(own_rows[half:], Y, down)

    attended = attend_sides(flags, q, kv_prev, kv_next, *centre)

    parity = lax.axis_index("ylo")
    split = attended.reshape(tl, zs, 2, -1)
    a_own = lax.dynamic_index_in_dim(split, parity, axis=2, keepdims=False).reshape(tl, -1)
    a_other = lax.dynamic_index_in_dim(split, 1 - parity, axis=2, keepdims=False).reshape(tl, -1)

    bands = lax.axis_size(ROWS)
    band = tl // bands
    me = lax.axis_index(ROWS)

    def project(start):
        own = lax.dynamic_slice_in_dim(a_own, start, band, axis=0)
        far = lax.dynamic_slice_in_dim(a_other, start, band, axis=0)
        part = jnp.dot(own, own_rows, preferred_element_type=jnp.float32)
        part = part + jnp.dot(far[:, :half], from_below, preferred_element_type=jnp.float32)
        return part + jnp.dot(far[:, half:], from_above, preferred_element_type=jnp.float32)

    sent = project((1 - me) * band).astype(jnp.bfloat16)
    got = lax.ppermute(sent, ROWS, [(0, 1), (1, 0)])
    kept = lax.optimization_barrier(project(me * band))
    projection = kept + got.astype(jnp.float32)
    mixed = (gate[0][None, :] * projection).astype(jnp.bfloat16)
    return mixed.reshape(1, 1, 1, 1, band, DOUT)


def solution(mesh):
    devices = mesh.devices.reshape(12, 2, 4, 4, 2)
    fine = Mesh(devices, ("z", "ylo", "x", "yhi", "core"))
    placed = (
        P(DP, TM, None, None, None, ROWS),
        P(DP, TM, None, None, None, None, ROWS),
        P(DP, TM, None, None, None),
        P((ROWS,) + DP, None),
        P(DP, None),
    )
    return jax.shard_map(
        local,
        mesh=fine,
        in_specs=placed,
        out_specs=P(DP, TM, None, None, ROWS, None),
        check_vma=False,
    )
```

```python
import functools

import jax
import jax.numpy as jnp
from jax import lax
from jax.experimental import pallas as pl
from jax.experimental.pallas import tpu as pltpu
from jax.sharding import Mesh
from jax.sharding import PartitionSpec as P

HD = 128
DOUT = 1536

DP = ("z", "ylo")
TM = ("x", "yhi")
ROWS = "core"
Y = ("ylo", "yhi")


def scores_of(q, k_ref, live):
    scale = float(HD) ** (-0.5)
    s = lax.dot_general(
        q, k_ref[...], (((1,), (1,)), ((), ())), preferred_element_type=jnp.float32
    ) * scale
    return jnp.where(live, s, -jnp.inf)


def centre_kernel(flags_ref, q_ref, k_ref, v_ref, m_ref, l_ref, acc_ref):
    live = flags_ref[1] > 0
    s = scores_of(q_ref[...], k_ref, live)
    top = jnp.max(s, axis=1, keepdims=True)
    p = jnp.where(live, jnp.exp(s - top), 0.0)
    m_ref[0] = jnp.where(live, top, -jnp.inf)
    l_ref[0] = p.sum(axis=1, keepdims=True)
    acc_ref[...] = jnp.dot(
        p.astype(jnp.bfloat16), v_ref[...], preferred_element_type=jnp.float32
    )


def side_kernel(flags_ref, q_ref, kp_ref, vp_ref, kn_ref, vn_ref, m_ref, l_ref, acc_ref, o_ref):
    q = q_ref[...]
    s_p = scores_of(q, kp_ref, flags_ref[0] > 0)
    s_n = scores_of(q, kn_ref, flags_ref[2] > 0)
    m_c = m_ref[0]
    top = jnp.maximum(
        m_c, jnp.maximum(jnp.max(s_p, axis=1, keepdims=True), jnp.max(s_n, axis=1, keepdims=True))
    )
    alpha = jnp.exp(m_c - top)
    p_p = jnp.exp(s_p - top)
    p_n = jnp.exp(s_n - top)
    total = alpha * l_ref[0] + p_p.sum(axis=1, keepdims=True) + p_n.sum(axis=1, keepdims=True)
    acc = alpha * acc_ref[...]
    acc = acc + jnp.dot(p_p.astype(jnp.bfloat16), vp_ref[...], preferred_element_type=jnp.float32)
    acc = acc + jnp.dot(p_n.astype(jnp.bfloat16), vn_ref[...], preferred_element_type=jnp.float32)
    o_ref[...] = (acc / total).astype(o_ref.dtype)


def split_kernel(kv_ref, o_ref):
    o_ref[...] = jnp.swapaxes(kv_ref[...], 0, 1)


def split_keys_values(kv):
    tl, _, width = kv.shape
    return pl.pallas_call(
        split_kernel,
        in_specs=[pl.BlockSpec(memory_space=pltpu.VMEM)],
        out_specs=pl.BlockSpec(memory_space=pltpu.VMEM),
        out_shape=jax.ShapeDtypeStruct((2, tl, width), kv.dtype),
        cost_estimate=pl.CostEstimate(flops=0, transcendentals=0, bytes_accessed=4 * tl * width * 2),
    )(kv)


def attend_centre(flags, q, kv_own):
    tl, width = q.shape
    heads = width // HD
    k_spec = pl.BlockSpec((None, tl, HD), lambda h, f: (0, 0, h))
    v_spec = pl.BlockSpec((None, tl, HD), lambda h, f: (1, 0, h))
    q_spec = pl.BlockSpec((tl, HD), lambda h, f: (0, h))
    stat_spec = pl.BlockSpec((1, tl, 1), lambda h, f: (h, 0, 0))
    stat_shape = jax.ShapeDtypeStruct((heads, tl, 1), jnp.float32)
    tile_flops = heads * 2 * 2 * tl * tl * HD
    m_c, l_c, acc_c = pl.pallas_call(
        centre_kernel,
        grid_spec=pltpu.PrefetchScalarGridSpec(
            num_scalar_prefetch=1,
            grid=(heads,),
            in_specs=[q_spec, k_spec, v_spec],
            out_specs=[stat_spec, stat_spec, q_spec],
        ),
        out_shape=[stat_shape, stat_shape, jax.ShapeDtypeStruct((tl, width), jnp.float32)],
        cost_estimate=pl.CostEstimate(
            flops=tile_flops,
            transcendentals=heads * tl * tl,
            bytes_accessed=tl * width * 2 * 3 + tl * width * 4,
        ),
    )(flags, q, kv_own, kv_own)
    return m_c, l_c, acc_c


def step_kernel(flag_idx, final, flags_ref, q_ref, k_ref, v_ref, m_ref, l_ref, acc_ref, *outs):
    s = scores_of(q_ref[...], k_ref, flags_ref[flag_idx] > 0)
    m_c = m_ref[0]
    top = jnp.maximum(m_c, jnp.max(s, axis=1, keepdims=True))
    alpha = jnp.exp(m_c - top)
    p = jnp.exp(s - top)
    total = alpha * l_ref[0] + p.sum(axis=1, keepdims=True)
    acc = alpha * acc_ref[...] + jnp.dot(
        p.astype(jnp.bfloat16), v_ref[...], preferred_element_type=jnp.float32
    )
    if final:
        outs[0][...] = (acc / total).astype(outs[0].dtype)
    else:
        outs[0][0] = top
        outs[1][0] = total
        outs[2][...] = acc


def attend_step(flags, q, kv_side, m_c, l_c, acc_c, flag_idx, final):
    tl, width = q.shape
    heads = width // HD
    k_spec = pl.BlockSpec((None, tl, HD), lambda h, f: (0, 0, h))
    v_spec = pl.BlockSpec((None, tl, HD), lambda h, f: (1, 0, h))
    q_spec = pl.BlockSpec((tl, HD), lambda h, f: (0, h))
    stat_spec = pl.BlockSpec((1, tl, 1), lambda h, f: (h, 0, 0))
    stat_shape = jax.ShapeDtypeStruct((heads, tl, 1), jnp.float32)
    if final:
        out_specs = q_spec
        out_shape = jax.ShapeDtypeStruct((tl, width), jnp.bfloat16)
    else:
        out_specs = [stat_spec, stat_spec, q_spec]
        out_shape = [stat_shape, stat_shape, jax.ShapeDtypeStruct((tl, width), jnp.float32)]
    tile_flops = heads * 2 * 2 * tl * tl * HD
    return pl.pallas_call(
        functools.partial(step_kernel, flag_idx, final),
        grid_spec=pltpu.PrefetchScalarGridSpec(
            num_scalar_prefetch=1,
            grid=(heads,),
            in_specs=[q_spec, k_spec, v_spec, stat_spec, stat_spec, q_spec],
            out_specs=out_specs,
        ),
        out_shape=out_shape,
        cost_estimate=pl.CostEstimate(
            flops=tile_flops,
            transcendentals=heads * tl * tl,
            bytes_accessed=tl * width * 2 * 3 + tl * width * 8,
        ),
    )(flags, q, kv_side, kv_side, m_c, l_c, acc_c)


def local(queries, keys_values, window_offsets, out_weight, gate):
    tl = queries.shape[4]
    all_time = lax.axis_size(TM)
    time_now = lax.axis_index(TM)

    forward = [(i, i + 1) for i in range(all_time - 1)]
    backward = [(i + 1, i) for i in range(all_time - 1)]
    kv = split_keys_values(keys_values[0, 0, 0, 0])
    kv_prev = lax.ppermute(kv, TM, forward)
    kv_next = lax.ppermute(kv, TM, backward)

    zs = lax.axis_size("z")
    spread = jnp.broadcast_to(out_weight[None], (zs,) + out_weight.shape)
    spread, kv = lax.optimization_barrier((spread, kv))
    own_rows = lax.all_to_all(spread, "z", 0, 0, tiled=True).reshape(-1, out_weight.shape[1])

    offsets = window_offsets[0, 0, 0, 0]
    near_t = time_now + offsets // 9 - 1
    same_hw = (offsets // 3 % 3 == 1) & (offsets % 3 == 1)
    inside = same_hw & (near_t >= 0) & (near_t < all_time)
    deltas = jnp.array([-1, 0, 1], jnp.int32)
    hit = inside[None, :] & (near_t[None, :] == time_now + deltas[:, None])
    flags = jnp.any(hit, axis=1).astype(jnp.int32)

    ys = lax.axis_size(Y)
    his = lax.axis_size("yhi")
    slot = [(y % 2) * his + y // 2 for y in range(ys)]
    up = [(slot[y], slot[(y + 1) % ys]) for y in range(ys)]
    down = [(slot[y], slot[(y - 1) % ys]) for y in range(ys)]
    half = own_rows.shape[0] // 2
    q = queries[0, 0, 0, 0]
    centre = attend_centre(flags, q, kv)
    kv_prev, centre = lax.optimization_barrier((kv_prev, centre))
    after_prev = attend_step(flags, q, kv_prev, *centre, 0, False)
    own_rows, kv_next, after_prev = lax.optimization_barrier((own_rows, kv_next, after_prev))
    from_below = lax.ppermute(own_rows[:half], Y, up)
    from_above = lax.ppermute(own_rows[half:], Y, down)

    attended = attend_step(flags, q, kv_next, *after_prev, 2, True)

    parity = lax.axis_index("ylo")
    split = attended.reshape(tl, zs, 2, -1)
    a_own = lax.dynamic_index_in_dim(split, parity, axis=2, keepdims=False).reshape(tl, -1)
    a_other = lax.dynamic_index_in_dim(split, 1 - parity, axis=2, keepdims=False).reshape(tl, -1)

    bands = lax.axis_size(ROWS)
    band = tl // bands
    me = lax.axis_index(ROWS)

    def project(start):
        own = lax.dynamic_slice_in_dim(a_own, start, band, axis=0)
        far = lax.dynamic_slice_in_dim(a_other, start, band, axis=0)
        part = jnp.dot(own, own_rows, preferred_element_type=jnp.float32)
        part = part + jnp.dot(far[:, :half], from_below, preferred_element_type=jnp.float32)
        return part + jnp.dot(far[:, half:], from_above, preferred_element_type=jnp.float32)

    sent = project((1 - me) * band).astype(jnp.bfloat16)
    got = lax.ppermute(sent, ROWS, [(0, 1), (1, 0)])
    kept = lax.optimization_barrier(project(me * band))
    projection = kept + got.astype(jnp.float32)
    mixed = (gate[0][None, :] * projection).astype(jnp.bfloat16)
    return mixed.reshape(1, 1, 1, 1, band, DOUT)


def solution(mesh):
    devices = mesh.devices.reshape(12, 2, 4, 4, 2)
    fine = Mesh(devices, ("z", "ylo", "x", "yhi", "core"))
    placed = (
        P(DP, TM, None, None, None, ROWS),
        P(DP, TM, None, None, None, None, ROWS),
        P(DP, TM, None, None, None),
        P((ROWS,) + DP, None),
        P(DP, None),
    )
    return jax.shard_map(
        local,
        mesh=fine,
        in_specs=placed,
        out_specs=P(DP, TM, None, None, ROWS, None),
        check_vma=False,
    )
```

```python
import functools

import jax
import jax.numpy as jnp
from jax import lax
from jax.experimental import pallas as pl
from jax.experimental.pallas import tpu as pltpu
from jax.sharding import Mesh
from jax.sharding import PartitionSpec as P

HD = 128
DOUT = 1536

DP = ("z", "ylo")
TM = ("x", "yhi")
ROWS = "core"
Y = ("ylo", "yhi")


def scores_of(q, k_ref, live):
    scale = float(HD) ** (-0.5)
    s = lax.dot_general(
        q, k_ref[...], (((1,), (1,)), ((), ())), preferred_element_type=jnp.float32
    ) * scale
    return jnp.where(live, s, -jnp.inf)


def centre_kernel(flags_ref, q_ref, k_ref, v_ref, m_ref, l_ref, acc_ref):
    live = flags_ref[1] > 0
    s = scores_of(q_ref[...], k_ref, live)
    top = jnp.max(s, axis=1, keepdims=True)
    p = jnp.where(live, jnp.exp(s - top), 0.0)
    m_ref[0] = jnp.where(live, top, -jnp.inf)
    l_ref[0] = p.sum(axis=1, keepdims=True)
    acc_ref[...] = jnp.dot(
        p.astype(jnp.bfloat16), v_ref[...], preferred_element_type=jnp.float32
    )


def side_kernel(flags_ref, q_ref, kp_ref, vp_ref, kn_ref, vn_ref, m_ref, l_ref, acc_ref, o_ref):
    q = q_ref[...]
    s_p = scores_of(q, kp_ref, flags_ref[0] > 0)
    s_n = scores_of(q, kn_ref, flags_ref[2] > 0)
    m_c = m_ref[0]
    top = jnp.maximum(
        m_c, jnp.maximum(jnp.max(s_p, axis=1, keepdims=True), jnp.max(s_n, axis=1, keepdims=True))
    )
    alpha = jnp.exp(m_c - top)
    p_p = jnp.exp(s_p - top)
    p_n = jnp.exp(s_n - top)
    total = alpha * l_ref[0] + p_p.sum(axis=1, keepdims=True) + p_n.sum(axis=1, keepdims=True)
    acc = alpha * acc_ref[...]
    acc = acc + jnp.dot(p_p.astype(jnp.bfloat16), vp_ref[...], preferred_element_type=jnp.float32)
    acc = acc + jnp.dot(p_n.astype(jnp.bfloat16), vn_ref[...], preferred_element_type=jnp.float32)
    o_ref[...] = (acc / total).astype(o_ref.dtype)


def split_kernel(kv_ref, o_ref):
    o_ref[...] = jnp.swapaxes(kv_ref[...], 0, 1)


def split_keys_values(kv):
    tl, _, width = kv.shape
    return pl.pallas_call(
        split_kernel,
        in_specs=[pl.BlockSpec(memory_space=pltpu.VMEM)],
        out_specs=pl.BlockSpec(memory_space=pltpu.VMEM),
        out_shape=jax.ShapeDtypeStruct((2, tl, width), kv.dtype),
        cost_estimate=pl.CostEstimate(flops=0, transcendentals=0, bytes_accessed=4 * tl * width * 2),
    )(kv)


def attend_centre(flags, q, kv_own):
    tl, width = q.shape
    heads = width // HD
    k_spec = pl.BlockSpec((None, tl, HD), lambda h, f: (0, 0, h))
    v_spec = pl.BlockSpec((None, tl, HD), lambda h, f: (1, 0, h))
    q_spec = pl.BlockSpec((tl, HD), lambda h, f: (0, h))
    stat_spec = pl.BlockSpec((1, tl, 1), lambda h, f: (h, 0, 0))
    stat_shape = jax.ShapeDtypeStruct((heads, tl, 1), jnp.float32)
    tile_flops = heads * 2 * 2 * tl * tl * HD
    m_c, l_c, acc_c = pl.pallas_call(
        centre_kernel,
        grid_spec=pltpu.PrefetchScalarGridSpec(
            num_scalar_prefetch=1,
            grid=(heads,),
            in_specs=[q_spec, k_spec, v_spec],
            out_specs=[stat_spec, stat_spec, q_spec],
        ),
        out_shape=[stat_shape, stat_shape, jax.ShapeDtypeStruct((tl, width), jnp.float32)],
        cost_estimate=pl.CostEstimate(
            flops=tile_flops,
            transcendentals=heads * tl * tl,
            bytes_accessed=tl * width * 2 * 3 + tl * width * 4,
        ),
    )(flags, q, kv_own, kv_own)
    return m_c, l_c, acc_c


def attend_sides(flags, q, kv_prev, kv_next, m_c, l_c, acc_c):
    tl, width = q.shape
    heads = width // HD
    k_spec = pl.BlockSpec((None, tl, HD), lambda h, f: (0, 0, h))
    v_spec = pl.BlockSpec((None, tl, HD), lambda h, f: (1, 0, h))
    q_spec = pl.BlockSpec((tl, HD), lambda h, f: (0, h))
    stat_spec = pl.BlockSpec((1, tl, 1), lambda h, f: (h, 0, 0))
    tile_flops = heads * 2 * 2 * tl * tl * HD
    return pl.pallas_call(
        side_kernel,
        grid_spec=pltpu.PrefetchScalarGridSpec(
            num_scalar_prefetch=1,
            grid=(heads,),
            in_specs=[q_spec, k_spec, v_spec, k_spec, v_spec, stat_spec, stat_spec, q_spec],
            out_specs=q_spec,
        ),
        out_shape=jax.ShapeDtypeStruct((tl, width), jnp.bfloat16),
        cost_estimate=pl.CostEstimate(
            flops=2 * tile_flops,
            transcendentals=2 * heads * tl * tl,
            bytes_accessed=tl * width * 2 * 6 + tl * width * 4,
        ),
    )(flags, q, kv_prev, kv_prev, kv_next, kv_next, m_c, l_c, acc_c)


def local(queries, keys_values, window_offsets, out_weight, gate):
    tl = queries.shape[4]
    all_time = lax.axis_size(TM)
    time_now = lax.axis_index(TM)

    forward = [(i, i + 1) for i in range(all_time - 1)]
    backward = [(i + 1, i) for i in range(all_time - 1)]
    kv = split_keys_values(keys_values[0, 0, 0, 0])
    kv_prev = lax.ppermute(kv, TM, forward)
    kv_next = lax.ppermute(kv, TM, backward)

    zs = lax.axis_size("z")
    spread = jnp.broadcast_to(out_weight[None], (zs,) + out_weight.shape)
    spread, kv = lax.optimization_barrier((spread, kv))
    own_rows = lax.all_to_all(spread, "z", 0, 0, tiled=True).reshape(-1, out_weight.shape[1])

    offsets = window_offsets[0, 0, 0, 0]
    near_t = time_now + offsets // 9 - 1
    same_hw = (offsets // 3 % 3 == 1) & (offsets % 3 == 1)
    inside = same_hw & (near_t >= 0) & (near_t < all_time)
    deltas = jnp.array([-1, 0, 1], jnp.int32)
    hit = inside[None, :] & (near_t[None, :] == time_now + deltas[:, None])
    flags = jnp.any(hit, axis=1).astype(jnp.int32)

    ys = lax.axis_size(Y)
    his = lax.axis_size("yhi")
    slot = [(y % 2) * his + y // 2 for y in range(ys)]
    up = [(slot[y], slot[(y + 1) % ys]) for y in range(ys)]
    down = [(slot[y], slot[(y - 1) % ys]) for y in range(ys)]
    half = own_rows.shape[0] // 2
    q = queries[0, 0, 0, 0]
    centre = attend_centre(flags, q, kv)
    own_rows, kv_prev, kv_next, centre = lax.optimization_barrier(
        (own_rows, kv_prev, kv_next, centre)
    )
    from_below = lax.ppermute(own_rows[:half], Y, up)
    from_above = lax.ppermute(own_rows[half:], Y, down)

    attended = attend_sides(flags, q, kv_prev, kv_next, *centre)

    parity = lax.axis_index("ylo")
    split = attended.reshape(tl, zs, 2, -1)
    a_own = lax.dynamic_index_in_dim(split, parity, axis=2, keepdims=False).reshape(tl, -1)
    a_other = lax.dynamic_index_in_dim(split, 1 - parity, axis=2, keepdims=False).reshape(tl, -1)

    bands = lax.axis_size(ROWS)
    band = tl // bands
    me = lax.axis_index(ROWS)

    def near(start):
        own = lax.dynamic_slice_in_dim(a_own, start, band, axis=0)
        return jnp.dot(own, own_rows, preferred_element_type=jnp.float32)

    def far(start, part):
        other = lax.dynamic_slice_in_dim(a_other, start, band, axis=0)
        part = part + jnp.dot(other[:, :half], from_below, preferred_element_type=jnp.float32)
        return part + jnp.dot(other[:, half:], from_above, preferred_element_type=jnp.float32)

    near_sent = near((1 - me) * band)
    near_kept = near(me * band)
    near_sent, near_kept, from_below, from_above = lax.optimization_barrier(
        (near_sent, near_kept, from_below, from_above)
    )
    sent = far((1 - me) * band, near_sent).astype(jnp.bfloat16)
    got = lax.ppermute(sent, ROWS, [(0, 1), (1, 0)])
    kept = lax.optimization_barrier(far(me * band, near_kept))
    projection = kept + got.astype(jnp.float32)
    mixed = (gate[0][None, :] * projection).astype(jnp.bfloat16)
    return mixed.reshape(1, 1, 1, 1, band, DOUT)


def solution(mesh):
    devices = mesh.devices.reshape(12, 2, 4, 4, 2)
    fine = Mesh(devices, ("z", "ylo", "x", "yhi", "core"))
    placed = (
        P(DP, TM, None, None, None, ROWS),
        P(DP, TM, None, None, None, None, ROWS),
        P(DP, TM, None, None, None),
        P((ROWS,) + DP, None),
        P(DP, None),
    )
    return jax.shard_map(
        local,
        mesh=fine,
        in_specs=placed,
        out_specs=P(DP, TM, None, None, ROWS, None),
        check_vma=False,
    )
```
